128 devices in a mesh: lon: 8 (over z_lo, x), lat: 16 (over y, z_hi, core).
Axes of the slice: x: 4, y: 4, z: 4 (z_hi: 2, z_lo: 2; z = z_hi * 2 + z_lo), core: 2. Of those that a mesh axis runs over, the one named last changes fastest.
Arguments:
- adjoint: float32 [4, 10, 1024, 4096], P(None, None, 'lat', 'lon'), may hold values from -6 to 6
- trajectory: float32 [4, 10, 1024, 4096], P(None, None, 'lat', 'lon'), may hold values from -6 to 6
- diffusivity: float32 [10, 1024, 4096], P(None, 'lat', 'lon'), may hold values from 0.06 to 0.24
- land_mask: int32 [10, 1024, 4096], P(None, 'lat', 'lon'), may hold values 0 or 1
- coriolis: float32 [1024], P('lat'), may hold values from -0.3 to 0.3
- obs_values: float32 [65536, 128], P(('lon', 'lat')), may hold values from -6 to 6
- obs_weight: float32 [65536], P(('lon', 'lat')), may hold values from 0.5 to 4
- obs_owner: int32 [65536, 1], P(('lon', 'lat')), may hold values from 0 to 127; in each aligned block of 512 rows (0 to 511, 512 to 1023, ...) at most 8 rows name the same one
- obs_offset: int32 [65536], P(('lon', 'lat')), may hold values from 0 to 10239
- fold_partner: int32 [4096], P('lon'), may hold values from 0 to 4095, as said below
Outputs:
- adjoint_out: float32 [4, 10, 1024, 4096], P(None, None, 'lat', 'lon')
The draws below stay inside these ranges and needn't reach their ends.
Inputs may be any that keep to these rules, and one draw needn't show every extreme that they name: `obs_owner`: in the rows of one device no owner is named by more than 8 rows, a bound that some block reaches. fold_partner is the mirror of the tripolar fold: fold_partner[i] = (4095 - i + o) modulo 4096 for one even offset o.
All inputs are finite; a program needn't handle non-finite values. No bound on the sum of `land_mask` on one device may be relied on, other than what follows from the above.
Results may differ from the reference program's by a relative error of at most 0.000059.
Values sent between devices are 32-bit elements; how exact they have to be, the bound alone decides.
No kernel may reach another device: no remote copies, remote signals or barrier semaphores. Data moves between devices by JAX's collectives and lax.ppermute only.
A program may use at most 320 MiB of HBM per device.

```python
import math
import jax
import jax.numpy as jnp
import numpy as np

FIELDS = 4
LEV = 10
NSUB = 3
SEG = 128
CAP = 8
CX = 512
CY = 64
NX = 4096
NY = 1024
OBS_DEV = 512
OBS_ROWS = 65536
TILE_ROWS = 10240
N_LAT = 16
DEVICES = 128


def draw_fold_partner(key, part):
    offset_half = jax.random.randint(key, (), 0, NX // 2).astype(jnp.int32)
    longitudes = jnp.arange(NX, dtype=jnp.int32)
    partner = (NX - 1 - longitudes + 2 * offset_half) % NX
    return partner.astype(jnp.int32)


def plant(result, key, least, high):
    extent = result.shape
    index_at = [jax.random.randint(jax.random.fold_in(key, axis), (), 0, extent[axis]) for axis in range(len(extent))]
    result = result.at[tuple(index_at)].set(least)
    longest = extent.index(max(extent))
    index_at[longest] = (index_at[longest] + 1) % extent[longest]
    return result.at[tuple(index_at)].set(high)


def block_levels(key, dims, shards, low, largest):
    def one(axis_at, parts):
        heights = jax.random.uniform(jax.random.fold_in(jax.random.fold_in(key, 6), axis_at), (parts,), jnp.float32, low / len(shards), largest / len(shards))
        return jnp.repeat(jnp.exp(heights), dims[axis_at] // parts).reshape((-1,) + (1,) * (len(dims) - axis_at - 1))

    loudness = one(*shards[0])
    for cut in shards[1:]:
        loudness = loudness * one(*cut)
    return loudness


def routed_block(key, own, number, rows, number_of, top, bound, skew):
    sequence = jax.random.permutation(key, number_of)
    packed, common = portions_of(number_of, rows * top, bound, skew, True), portions_of(number_of, rows * top, bound, skew, False)
    places = jnp.arange(number_of)

    def named(sizes, offset_by):
        used = int((sizes > 0).sum())
        fixed = max(1, used // 4)
        shifted = fixed + (places - fixed + offset_by * (used - fixed)) % max(1, number_of - fixed)
        return jnp.zeros((number_of,), jnp.int32).at[sequence[jnp.where(places < fixed, places, shifted)]].set(jnp.asarray(sizes, jnp.int32))

    sizes = jnp.where(number % 4 == 0, named(packed, number // 4), named(common, number - number // 4 - 1))
    mixed = jax.random.permutation(jax.random.fold_in(own, 3), number_of)
    giver, receiver = mixed[0:number_of // 2 * 2:2], mixed[1:number_of // 2 * 2:2]
    slack = jnp.minimum(sizes[giver] - 1, bound - sizes[receiver]) // 2
    slack = jnp.where((giver == sequence[0]) | (receiver == sequence[0]) | (sizes[receiver] == 0), 0, jnp.maximum(slack, 0))
    shifted = jax.random.randint(jax.random.fold_in(own, 4), (number_of // 2,), 0, 1 << 20) % (slack + 1)
    sizes = sizes.at[giver].add(-shifted).at[receiver].add(shifted)
    members = jnp.searchsorted(jnp.cumsum(sizes), jnp.arange(rows * top), side="right").astype(jnp.int32)
    grid = members.reshape(top, rows).T
    grid = grid[jax.random.permutation(jax.random.fold_in(own, 1), rows)]
    offset_by = jax.random.randint(jax.random.fold_in(own, 2), (rows, 1), 0, top)
    return jnp.take_along_axis(grid, (jnp.arange(top)[None, :] + offset_by) % top, axis=1)


def portions_of(amount, total, limit, slope, full):
    weights = [(1 << 20) // math.isqrt(rank ** slope) + 1 for rank in range(1, amount + 1)]
    largest = limit if full else min(limit, max(-(-total // amount), total * weights[0] // sum(weights)))
    least = 1 if total - largest >= amount - 1 else 0
    counts, spare = [largest] + [least] * (amount - 1), total - largest - least * (amount - 1)
    while spare > 0:
        movable = [i for i in range(1, amount) if counts[i] < largest] or [i for i in range(1, amount) if counts[i] < limit]
        pool, left = sum([weights[i] for i in movable]), spare
        for i in movable:
            more = min(limit - counts[i], max(1, left * weights[i] // pool), spare)
            counts[i] = counts[i] + more
            spare = spare - more
    return np.array(counts)


def scatter_about(stream_key, extent, deviation, bound, cuts=(), kind=jnp.bfloat16):
    loudness = block_levels(stream_key, extent, cuts, -0.22, 0.18) if cuts else 1.0
    result = jax.random.normal(stream_key, extent, jnp.float32) * deviation * loudness
    return jnp.minimum(jnp.maximum(result, -bound), bound).astype(kind)


def setup_inputs(seed: int = 0) -> dict:
    seeds = jax.random.split(jax.random.key(seed), 11)
    adjoint = scatter_about(seeds[0], (FIELDS, LEV, NY, NX), 1.0, 6.0, ((2, 16), (3, 8)), jnp.float32)
    trajectory = scatter_about(seeds[1], (FIELDS, LEV, NY, NX), 1.0, 6.0, ((2, 16), (3, 8)), jnp.float32)
    diffusivity = jnp.clip(jnp.exp(math.log(0.24) - 1.3862944 * jax.random.uniform(seeds[2], (LEV, NY, NX), jnp.float32) ** block_levels(seeds[2], (LEV, NY, NX), ((1, 16), (2, 8)), -0.2, 0.2)), 0.06, 0.24)
    land_mask = plant((jax.random.randint(seeds[3], (LEV, NY, NX), 0, 4) < 3).astype(jnp.int32), jax.random.fold_in(seeds[3], 1), 0, 1)
    coriolis = jnp.clip(jax.random.uniform(seeds[4], (NY,), jnp.float32, -0.3, 0.3) * block_levels(seeds[4], (NY,), ((0, 16),), -0.4, 0.0), -0.3, 0.3)
    obs_values = scatter_about(seeds[5], (OBS_ROWS, SEG), 1.0, 6.0, ((0, 128),), jnp.float32)
    obs_weight = jnp.clip(jnp.exp(math.log(4.0) - 2.0794415 * jax.random.uniform(seeds[6], (OBS_ROWS,), jnp.float32) ** block_levels(seeds[6], (OBS_ROWS,), ((0, 128),), -0.2, 0.2)), 0.5, 4.0)
    obs_owner_keys = jax.random.split(jax.random.fold_in(seeds[7], 1), OBS_ROWS // OBS_DEV)
    obs_owner_turns = jax.random.permutation(jax.random.fold_in(seeds[7], 3), OBS_ROWS // OBS_DEV)
    obs_owner = jax.vmap(lambda own, number: routed_block(jax.random.fold_in(seeds[7], 2), own, number, OBS_DEV, DEVICES, 1, CAP, 2))(obs_owner_keys, obs_owner_turns).reshape((OBS_ROWS, 1))
    obs_offset = plant(jax.random.randint(seeds[8], (OBS_ROWS,), 0, TILE_ROWS), jax.random.fold_in(seeds[8], 1), 0, TILE_ROWS - 1).astype(jnp.int32)
    fold_partner = draw_fold_partner(jax.random.fold_in(seeds[10], 71), 0)
    return {"adjoint": adjoint, "trajectory": trajectory, "diffusivity": diffusivity, "land_mask": land_mask, "coriolis": coriolis, "obs_values": obs_values, "obs_weight": obs_weight, "obs_owner": obs_owner, "obs_offset": obs_offset, "fold_partner": fold_partner}


def reference(adjoint, trajectory, diffusivity, land_mask, coriolis, obs_values, obs_weight, obs_owner, obs_offset, fold_partner):
    wet_cells = land_mask.astype(jnp.float32)
    field_sign = jnp.array([1.0, 1.0, -1.0, -1.0], jnp.float32).reshape(4, 1, 1, 1)
    work_state = adjoint * wet_cells[None]
    for sweep_index in range(NSUB):
        ghost_rows = field_sign * jnp.take(work_state[:, :, NY - 1:NY, :], fold_partner, axis=3)
        northern = jnp.concatenate([work_state[:, :, 1:, :], ghost_rows], axis=2)
        southern = jnp.concatenate([jnp.zeros_like(work_state[:, :, :1, :]), work_state[:, :, :-1, :]], axis=2)
        eastern = jnp.roll(work_state, -1, axis=3)
        western = jnp.roll(work_state, 1, axis=3)
        laplace = eastern + western + northern + southern - 4.0 * work_state
        work_state = work_state + diffusivity[None] * laplace
    rotation = coriolis[:, None]
    adjoint_u = work_state[2] - rotation * work_state[3]
    adjoint_v = work_state[3] + rotation * work_state[2]
    mixed = jnp.stack([work_state[0], work_state[1], adjoint_u, adjoint_v])
    segments = CX // SEG
    owner_index = obs_owner[:, 0]
    lon_tile = owner_index // N_LAT
    lat_band = owner_index % N_LAT
    seg_local = obs_offset % segments
    rest_index = obs_offset // segments
    row_local = rest_index % CY
    layer_index = rest_index // CY
    glob_row = (lat_band * CY + row_local).astype(jnp.int32)
    glob_seg = (lon_tile * segments + seg_local).astype(jnp.int32)
    traj_view = trajectory.reshape(FIELDS * LEV, NY, NX // SEG, SEG)
    misfit = obs_weight[:, None] * (traj_view[layer_index, glob_row, glob_seg] - obs_values)
    forcing = jnp.zeros_like(traj_view).at[layer_index, glob_row, glob_seg].add(misfit)
    forcing = forcing.reshape(FIELDS, LEV, NY, NX)
    return wet_cells[None] * (mixed + forcing)
```

```python
import functools

import jax
import jax.numpy as jnp
from jax import lax
from jax.experimental import pallas as pl
from jax.experimental.pallas import tpu as pltpu
from jax.sharding import PartitionSpec as P

NSUB = 3
CAP = 8
HALO = 3
PAD_ROWS = 8
PAD_LANES = 128


def exact_dot(left, right, left_dim):
    return lax.dot_general(
        left,
        right,
        (((left_dim,), (0,)), ((), ())),
        precision=lax.Precision.HIGHEST,
        preferred_element_type=jnp.float32,
    )


def mix_kernel(adj_ref, mask_ref, diff_ref, rows_ref, cols_ref, cor_ref, out_ref, xs, ds):
    fields = adj_ref.shape[0]
    h, w = adj_ref.shape[2], adj_ref.shape[3]
    hp, wp = xs.shape[1], xs.shape[2]
    wet = mask_ref[0].astype(jnp.float32)
    for f in range(fields):
        xs[f, 0:h, 0:w] = adj_ref[f, 0] * wet
        xs[f, h:hp, 0:w] = rows_ref[f, 0]
        xs[f, :, w:wp] = cols_ref[f, 0]
    ds[0:h, 0:w] = diff_ref[0]
    ds[h:hp, 0:w] = rows_ref[fields, 0]
    ds[:, w:wp] = cols_ref[fields, 0]
    d = ds[...]
    done = []
    for f in range(fields):
        x = xs[f]
        for _ in range(NSUB):
            east = pltpu.roll(x, wp - 1, 1)
            west = pltpu.roll(x, 1, 1)
            north = pltpu.roll(x, hp - 1, 0)
            south = pltpu.roll(x, 1, 0)
            x = x + d * (east + west + north + south - 4.0 * x)
        done.append(x[0:h, 0:w])
    rot = cor_ref[...]
    out_ref[0, 0] = wet * done[0]
    out_ref[1, 0] = wet * done[1]
    out_ref[2, 0] = wet * (done[2] - rot * done[3])
    out_ref[3, 0] = wet * (done[3] + rot * done[2])


def mix_call(adjoint, land_mask, diffusivity, rows5, cols5, coriolis):
    fields, levels, h, w = adjoint.shape
    hp, wp = h + PAD_ROWS, w + PAD_LANES
    return pl.pallas_call(
        mix_kernel,
        grid=(levels,),
        in_specs=[
            pl.BlockSpec((fields, 1, h, w), lambda k: (0, k, 0, 0)),
            pl.BlockSpec((1, h, w), lambda k: (k, 0, 0)),
            pl.BlockSpec((1, h, w), lambda k: (k, 0, 0)),
            pl.BlockSpec((fields + 1, 1, PAD_ROWS, w), lambda k: (0, k, 0, 0)),
            pl.BlockSpec((fields + 1, 1, hp, PAD_LANES), lambda k: (0, k, 0, 0)),
            pl.BlockSpec((h, 1), lambda k: (0, 0)),
        ],
        out_specs=pl.BlockSpec((fields, 1, h, w), lambda k: (0, k, 0, 0)),
        out_shape=jax.ShapeDtypeStruct(adjoint.shape, jnp.float32),
        scratch_shapes=[
            pltpu.VMEM((fields, hp, wp), jnp.float32),
            pltpu.VMEM((hp, wp), jnp.float32),
        ],
    )(adjoint, land_mask, diffusivity, rows5, cols5, coriolis.reshape(h, 1))


def fold_rows(top_msg, fold_partner, width):
    lon_count = lax.axis_size("lon")
    lat_count = lax.axis_size("lat")
    lon = lax.axis_index("lon")
    nx = lon_count * width
    first = lon * width
    offset = (fold_partner[0] + first - (nx - 1)) % nx
    shift_tiles = offset // width
    shift_in = offset % width
    top = lat_count - 1

    def branch(q):
        def run(msg):
            pairs_a, pairs_b = [], []
            for t in range(lon_count):
                src_a = (lon_count - 1 - t + q) % lon_count
                src_b = (src_a + 1) % lon_count
                pairs_a.append((src_a * lat_count + top, t * lat_count + top))
                pairs_b.append((src_b * lat_count + top, t * lat_count + top))
            got_a = lax.ppermute(msg, ("lon", "lat"), pairs_a)
            got_b = lax.ppermute(msg, ("lon", "lat"), pairs_b)
            return jnp.concatenate([got_a, got_b], axis=2)

        return run

    both = lax.switch(shift_tiles, [branch(q) for q in range(lon_count)], top_msg)
    window = lax.dynamic_slice_in_dim(both, shift_in, width, axis=2)
    return window[:, ::-1, ::-1]


def per_device(
    adjoint,
    trajectory,
    diffusivity,
    land_mask,
    coriolis,
    obs_values,
    obs_weight,
    obs_owner,
    obs_offset,
    fold_partner,
):
    fields, levels, h, w = adjoint.shape
    lat_count = lax.axis_size("lat")
    lon_count = lax.axis_size("lon")
    lat = lax.axis_index("lat")
    n_work = fields * levels
    sign = jnp.array([1.0, 1.0, -1.0, -1.0], jnp.float32).reshape(fields, 1, 1, 1)

    def edge(rows):
        wet_rows = land_mask[:, rows, :].astype(jnp.float32)
        work_rows = adjoint[:, :, rows, :] * wet_rows[None]
        return work_rows, diffusivity[:, rows, :]

    top_work, top_diff = edge(slice(h - HALO, h))
    bot_work, bot_diff = edge(slice(0, HALO))
    top_msg = jnp.concatenate([top_work.reshape(n_work, HALO, w), top_diff], axis=0)
    bot_msg = jnp.concatenate([bot_work.reshape(n_work, HALO, w), bot_diff], axis=0)
    up = [(i, i + 1) for i in range(lat_count - 1)]
    down = [(i + 1, i) for i in range(lat_count - 1)]
    from_below = lax.ppermute(top_msg, "lat", up)
    from_above = lax.ppermute(bot_msg, "lat", down)
    signed_top = jnp.concatenate(
        [(top_work * sign).reshape(n_work, HALO, w), top_diff], axis=0
    )
    folded = fold_rows(signed_top, fold_partner, w)
    north = jnp.where(lat == lat_count - 1, folded, from_above)
    gap = jnp.zeros((n_work + levels, PAD_ROWS - 2 * HALO, w), jnp.float32)
    rows_all = jnp.concatenate([north, gap, from_below], axis=1)
    rows5 = rows_all.reshape(fields + 1, levels, PAD_ROWS, w)

    work_first = adjoint[:, :, :, :HALO] * land_mask[None, :, :, :HALO].astype(jnp.float32)
    work_last = adjoint[:, :, :, w - HALO :] * land_mask[None, :, :, w - HALO :].astype(jnp.float32)
    first = jnp.concatenate(
        [
            jnp.concatenate([work_first.reshape(n_work, h, HALO), diffusivity[:, :, :HALO]], 0),
            rows_all[:, :, :HALO],
        ],
        axis=1,
    )
    last = jnp.concatenate(
        [
            jnp.concatenate([work_last.reshape(n_work, h, HALO), diffusivity[:, :, w - HALO :]], 0),
            rows_all[:, :, w - HALO :],
        ],
        axis=1,
    )
    ring_west = [(i, (i - 1) % lon_count) for i in range(lon_count)]
    ring_east = [(i, (i + 1) % lon_count) for i in range(lon_count)]
    first_t = jnp.swapaxes(first, 1, 2)
    last_t = jnp.swapaxes(last, 1, 2)
    east_halo = jnp.swapaxes(lax.ppermute(first_t, "lon", ring_west), 1, 2)
    west_halo = jnp.swapaxes(lax.ppermute(last_t, "lon", ring_east), 1, 2)
    hp = h + PAD_ROWS
    middle = jnp.zeros((n_work + levels, hp, PAD_LANES - 2 * HALO), jnp.float32)
    cols5 = jnp.concatenate([east_halo, middle, west_halo], axis=2).reshape(
        fields + 1, levels, hp, PAD_LANES
    )

    mixed_wet = mix_call(adjoint, land_mask, diffusivity, rows5, cols5, coriolis)

    devices = lon_count * lat_count
    seg_width = obs_values.shape[1]
    rows_sent = obs_values.shape[0]
    owner_index = obs_owner[:, 0]
    one_hot = (owner_index[:, None] == jnp.arange(devices, dtype=jnp.int32)[None, :]).astype(
        jnp.bfloat16
    )
    row_ids = jnp.arange(rows_sent, dtype=jnp.int32)
    before = (row_ids[None, :] < row_ids[:, None]).astype(jnp.bfloat16)
    earlier = lax.dot_general(
        before, one_hot, (((1,), (0,)), ((), ())), preferred_element_type=jnp.float32
    )
    slot_index = jnp.sum(earlier * one_hot.astype(jnp.float32), axis=1).astype(jnp.int32)
    dest_index = owner_index * CAP + slot_index
    slot_ids = jnp.arange(devices * CAP, dtype=jnp.int32)
    placement = (dest_index[:, None] == slot_ids[None, :]).astype(jnp.float32)
    send_values = exact_dot(placement, obs_values, 0).reshape(devices, CAP, seg_width)
    meta = jnp.stack([obs_weight, obs_offset.astype(jnp.float32)], axis=1)
    send_meta = exact_dot(placement, meta, 0).reshape(devices, CAP, 2)
    send_meta = jnp.swapaxes(send_meta, 1, 2).reshape(devices, 2 * CAP)
    send_meta = jnp.pad(send_meta, ((0, 0), (0, seg_width - 2 * CAP)))
    send = jnp.concatenate([send_values.reshape(devices, CAP * seg_width), send_meta], axis=1)
    got = lax.all_to_all(send, ("lon", "lat"), split_axis=0, concat_axis=0, tiled=True)
    got_values = got[:, : CAP * seg_width].reshape(devices * CAP, seg_width)
    got_meta = got[:, CAP * seg_width : CAP * seg_width + 2 * CAP].reshape(devices, 2, CAP)
    got_weight = got_meta[:, 0, :].reshape(devices * CAP)
    got_offset = got_meta[:, 1, :].reshape(devices * CAP).astype(jnp.int32)

    segments = w // seg_width
    seg_local = got_offset % segments
    rest = got_offset // segments
    row_local = rest % h
    layer = rest // h
    index = jnp.stack([layer, row_local, seg_local * seg_width], axis=1)
    traj3 = trajectory.reshape(n_work, h, w)
    gdn = lax.GatherDimensionNumbers(
        offset_dims=(1,), collapsed_slice_dims=(0, 1), start_index_map=(0, 1, 2)
    )
    sampled = lax.gather(
        traj3, index, gdn, (1, 1, seg_width), mode=lax.GatherScatterMode.PROMISE_IN_BOUNDS
    )
    level_index = jnp.stack([layer % levels, row_local, seg_local * seg_width], axis=1)
    wet_rows = lax.gather(
        land_mask, level_index, gdn, (1, 1, seg_width), mode=lax.GatherScatterMode.PROMISE_IN_BOUNDS
    ).astype(jnp.float32)
    misfit = got_weight[:, None] * (sampled - got_values)
    sdn = lax.ScatterDimensionNumbers(
        update_window_dims=(1,), inserted_window_dims=(0, 1), scatter_dims_to_operand_dims=(0, 1, 2)
    )
    out3 = lax.scatter_add(
        mixed_wet.reshape(n_work, h, w),
        index,
        wet_rows * misfit,
        sdn,
        mode=lax.GatherScatterMode.PROMISE_IN_BOUNDS,
    )
    return out3.reshape(adjoint.shape)


def solution(mesh):
    return jax.shard_map(
        per_device,
        mesh=mesh,
        in_specs=(
            P(None, None, "lat", "lon"),
            P(None, None, "lat", "lon"),
            P(None, "lat", "lon"),
            P(None, "lat", "lon"),
            P("lat"),
            P(("lon", "lat"), None),
            P(("lon", "lat")),
            P(("lon", "lat"), None),
            P(("lon", "lat")),
            P("lon"),
        ),
        out_specs=P(None, None, "lat", "lon"),
        check_vma=False,
    )
```

```python
import functools

import jax
import jax.numpy as jnp
from jax import lax
from jax.experimental import pallas as pl
from jax.experimental.pallas import tpu as pltpu
from jax.sharding import PartitionSpec as P

NSUB = 3
CAP = 8
HALO = 3
PAD_ROWS = 8
PAD_LANES = 128


def exact_dot(left, right, left_dim):
    return lax.dot_general(
        left,
        right,
        (((left_dim,), (0,)), ((), ())),
        precision=lax.Precision.HIGHEST,
        preferred_element_type=jnp.float32,
    )


def mix_kernel(adj_ref, mask_ref, diff_ref, rows_ref, cols_ref, cor_ref, out_ref, xs, ds):
    fields = adj_ref.shape[0]
    h, w = adj_ref.shape[2], adj_ref.shape[3]
    hp, wp = xs.shape[1], xs.shape[2]
    wet = mask_ref[0].astype(jnp.float32)
    for f in range(fields):
        xs[f, 0:h, 0:w] = adj_ref[f, 0] * wet
        xs[f, h:hp, 0:w] = rows_ref[f, 0]
        xs[f, :, w:wp] = cols_ref[f, 0]
    ds[0:h, 0:w] = diff_ref[0]
    ds[h:hp, 0:w] = rows_ref[fields, 0]
    ds[:, w:wp] = cols_ref[fields, 0]
    d = ds[...]
    done = []
    for f in range(fields):
        x = xs[f]
        for _ in range(NSUB):
            east = pltpu.roll(x, wp - 1, 1)
            west = pltpu.roll(x, 1, 1)
            north = pltpu.roll(x, hp - 1, 0)
            south = pltpu.roll(x, 1, 0)
            x = x + d * (east + west + north + south - 4.0 * x)
        done.append(x[0:h, 0:w])
    rot = cor_ref[...]
    out_ref[0, 0] = wet * done[0]
    out_ref[1, 0] = wet * done[1]
    out_ref[2, 0] = wet * (done[2] - rot * done[3])
    out_ref[3, 0] = wet * (done[3] + rot * done[2])


def mix_call(adjoint, land_mask, diffusivity, rows5, cols5, coriolis):
    fields, levels, h, w = adjoint.shape
    hp, wp = h + PAD_ROWS, w + PAD_LANES
    return pl.pallas_call(
        mix_kernel,
        grid=(levels,),
        in_specs=[
            pl.BlockSpec((fields, 1, h, w), lambda k: (0, k, 0, 0)),
            pl.BlockSpec((1, h, w), lambda k: (k, 0, 0)),
            pl.BlockSpec((1, h, w), lambda k: (k, 0, 0)),
            pl.BlockSpec((fields + 1, 1, PAD_ROWS, w), lambda k: (0, k, 0, 0)),
            pl.BlockSpec((fields + 1, 1, hp, PAD_LANES), lambda k: (0, k, 0, 0)),
            pl.BlockSpec((h, 1), lambda k: (0, 0)),
        ],
        out_specs=pl.BlockSpec((fields, 1, h, w), lambda k: (0, k, 0, 0)),
        out_shape=jax.ShapeDtypeStruct(adjoint.shape, jnp.float32),
        scratch_shapes=[
            pltpu.VMEM((fields, hp, wp), jnp.float32),
            pltpu.VMEM((hp, wp), jnp.float32),
        ],
    )(adjoint, land_mask, diffusivity, rows5, cols5, coriolis.reshape(h, 1))


def obs_kernel(where_ref, weight_ref, vals_ref, traj_ref, mask_ref, base_ref, out_ref):
    out_ref[...] = base_ref[...]
    seg_width = vals_ref.shape[1]
    sub = lax.broadcasted_iota(jnp.int32, (8, seg_width), 0)

    def body(o, carry):
        first = pl.multiple_of(o * 8, 8)
        vals8 = vals_ref[pl.ds(first, 8), :]
        for j in range(8):
            i = first + j
            layer = where_ref[0, i]
            row = where_ref[1, i]
            col = pl.multiple_of(where_ref[2, i], seg_width)
            level = where_ref[3, i]
            tile = pl.multiple_of((row // 8) * 8, 8)
            rows = pl.ds(tile, 8)
            cols = pl.ds(col, seg_width)
            sampled = traj_ref[layer, rows, cols]
            misfit = weight_ref[i] * (sampled - vals8[j : j + 1, :])
            wet = mask_ref[level, rows, cols].astype(jnp.float32)
            hit = sub == row - tile
            cur = out_ref[layer, rows, cols]
            out_ref[layer, rows, cols] = cur + jnp.where(hit, wet * misfit, 0.0)
        return carry

    lax.fori_loop(0, vals_ref.shape[0] // 8, body, 0)


def obs_call(where, weight, values, traj3, land_mask, base3):
    whole = lambda shape: pl.BlockSpec(shape, lambda i, *_: (0,) * len(shape))
    return pl.pallas_call(
        obs_kernel,
        grid_spec=pltpu.PrefetchScalarGridSpec(
            num_scalar_prefetch=2,
            grid=(1,),
            in_specs=[
                whole(values.shape),
                whole(traj3.shape),
                whole(land_mask.shape),
                whole(base3.shape),
            ],
            out_specs=whole(base3.shape),
        ),
        out_shape=jax.ShapeDtypeStruct(base3.shape, jnp.float32),
        compiler_params=pltpu.CompilerParams(vmem_limit_bytes=60 * 1024 * 1024),
    )(where, weight, values, traj3, land_mask, base3)


def fold_rows(top_msg, fold_partner, width):
    lon_count = lax.axis_size("lon")
    lat_count = lax.axis_size("lat")
    lon = lax.axis_index("lon")
    nx = lon_count * width
    first = lon * width
    offset = (fold_partner[0] + first - (nx - 1)) % nx
    shift_tiles = offset // width
    shift_in = offset % width
    top = lat_count - 1

    def branch(q):
        def run(msg):
            pairs_a, pairs_b = [], []
            for t in range(lon_count):
                src_a = (lon_count - 1 - t + q) % lon_count
                src_b = (src_a + 1) % lon_count
                pairs_a.append((src_a * lat_count + top, t * lat_count + top))
                pairs_b.append((src_b * lat_count + top, t * lat_count + top))
            got_a = lax.ppermute(msg, ("lon", "lat"), pairs_a)
            got_b = lax.ppermute(msg, ("lon", "lat"), pairs_b)
            return jnp.concatenate([got_a, got_b], axis=2)

        return run

    both = lax.switch(shift_tiles, [branch(q) for q in range(lon_count)], top_msg)
    window = lax.dynamic_slice_in_dim(both, shift_in, width, axis=2)
    return window[:, ::-1, ::-1]


def per_device(
    adjoint,
    trajectory,
    diffusivity,
    land_mask,
    coriolis,
    obs_values,
    obs_weight,
    obs_owner,
    obs_offset,
    fold_partner,
):
    fields, levels, h, w = adjoint.shape
    lat_count = lax.axis_size("lat")
    lon_count = lax.axis_size("lon")
    lat = lax.axis_index("lat")
    n_work = fields * levels
    sign = jnp.array([1.0, 1.0, -1.0, -1.0], jnp.float32).reshape(fields, 1, 1, 1)

    def edge(rows):
        wet_rows = land_mask[:, rows, :].astype(jnp.float32)
        work_rows = adjoint[:, :, rows, :] * wet_rows[None]
        return work_rows, diffusivity[:, rows, :]

    top_work, top_diff = edge(slice(h - HALO, h))
    bot_work, bot_diff = edge(slice(0, HALO))
    top_msg = jnp.concatenate([top_work.reshape(n_work, HALO, w), top_diff], axis=0)
    bot_msg = jnp.concatenate([bot_work.reshape(n_work, HALO, w), bot_diff], axis=0)
    up = [(i, i + 1) for i in range(lat_count - 1)]
    down = [(i + 1, i) for i in range(lat_count - 1)]
    from_below = lax.ppermute(top_msg, "lat", up)
    from_above = lax.ppermute(bot_msg, "lat", down)
    signed_top = jnp.concatenate(
        [(top_work * sign).reshape(n_work, HALO, w), top_diff], axis=0
    )
    folded = fold_rows(signed_top, fold_partner, w)
    north = jnp.where(lat == lat_count - 1, folded, from_above)
    gap = jnp.zeros((n_work + levels, PAD_ROWS - 2 * HALO, w), jnp.float32)
    rows_all = jnp.concatenate([north, gap, from_below], axis=1)
    rows5 = rows_all.reshape(fields + 1, levels, PAD_ROWS, w)

    work_first = adjoint[:, :, :, :HALO] * land_mask[None, :, :, :HALO].astype(jnp.float32)
    work_last = adjoint[:, :, :, w - HALO :] * land_mask[None, :, :, w - HALO :].astype(jnp.float32)
    first = jnp.concatenate(
        [
            jnp.concatenate([work_first.reshape(n_work, h, HALO), diffusivity[:, :, :HALO]], 0),
            rows_all[:, :, :HALO],
        ],
        axis=1,
    )
    last = jnp.concatenate(
        [
            jnp.concatenate([work_last.reshape(n_work, h, HALO), diffusivity[:, :, w - HALO :]], 0),
            rows_all[:, :, w - HALO :],
        ],
        axis=1,
    )
    ring_west = [(i, (i - 1) % lon_count) for i in range(lon_count)]
    ring_east = [(i, (i + 1) % lon_count) for i in range(lon_count)]
    first_t = jnp.swapaxes(first, 1, 2)
    last_t = jnp.swapaxes(last, 1, 2)
    east_halo = jnp.swapaxes(lax.ppermute(first_t, "lon", ring_west), 1, 2)
    west_halo = jnp.swapaxes(lax.ppermute(last_t, "lon", ring_east), 1, 2)
    hp = h + PAD_ROWS
    middle = jnp.zeros((n_work + levels, hp, PAD_LANES - 2 * HALO), jnp.float32)
    cols5 = jnp.concatenate([east_halo, middle, west_halo], axis=2).reshape(
        fields + 1, levels, hp, PAD_LANES
    )

    mixed_wet = mix_call(adjoint, land_mask, diffusivity, rows5, cols5, coriolis)

    devices = lon_count * lat_count
    seg_width = obs_values.shape[1]
    rows_sent = obs_values.shape[0]
    owner_index = obs_owner[:, 0]
    one_hot = (owner_index[:, None] == jnp.arange(devices, dtype=jnp.int32)[None, :]).astype(
        jnp.bfloat16
    )
    row_ids = jnp.arange(rows_sent, dtype=jnp.int32)
    before = (row_ids[None, :] < row_ids[:, None]).astype(jnp.bfloat16)
    earlier = lax.dot_general(
        before, one_hot, (((1,), (0,)), ((), ())), preferred_element_type=jnp.float32
    )
    slot_index = jnp.sum(earlier * one_hot.astype(jnp.float32), axis=1).astype(jnp.int32)
    dest_index = owner_index * CAP + slot_index
    slot_ids = jnp.arange(devices * CAP, dtype=jnp.int32)
    placement = (dest_index[:, None] == slot_ids[None, :]).astype(jnp.float32)
    send_values = exact_dot(placement, obs_values, 0).reshape(devices, CAP, seg_width)
    meta = jnp.stack([obs_weight, obs_offset.astype(jnp.float32)], axis=1)
    send_meta = exact_dot(placement, meta, 0).reshape(devices, CAP, 2)
    send_meta = jnp.swapaxes(send_meta, 1, 2).reshape(devices, 2 * CAP)
    send_meta = jnp.pad(send_meta, ((0, 0), (0, seg_width - 2 * CAP)))
    send = jnp.concatenate([send_values.reshape(devices, CAP * seg_width), send_meta], axis=1)
    got = lax.all_to_all(send, ("lon", "lat"), split_axis=0, concat_axis=0, tiled=True)
    got_values = got[:, : CAP * seg_width].reshape(devices * CAP, seg_width)
    got_meta = got[:, CAP * seg_width : CAP * seg_width + 2 * CAP].reshape(devices, 2, CAP)
    got_weight = got_meta[:, 0, :].reshape(devices * CAP)
    got_offset = got_meta[:, 1, :].reshape(devices * CAP).astype(jnp.int32)

    segments = w // seg_width
    seg_local = got_offset % segments
    rest = got_offset // segments
    row_local = rest % h
    layer = rest // h
    where = jnp.stack([layer, row_local, seg_local * seg_width, layer % levels], axis=0)
    out3 = obs_call(
        where,
        got_weight,
        got_values,
        trajectory.reshape(n_work, h, w),
        land_mask,
        mixed_wet.reshape(n_work, h, w),
    )
    return out3.reshape(adjoint.shape)


def solution(mesh):
    return jax.shard_map(
        per_device,
        mesh=mesh,
        in_specs=(
            P(None, None, "lat", "lon"),
            P(None, None, "lat", "lon"),
            P(None, "lat", "lon"),
            P(None, "lat", "lon"),
            P("lat"),
            P(("lon", "lat"), None),
            P(("lon", "lat")),
            P(("lon", "lat"), None),
            P(("lon", "lat")),
            P("lon"),
        ),
        out_specs=P(None, None, "lat", "lon"),
        check_vma=False,
    )
```

```python
import functools

import jax
import jax.numpy as jnp
from jax import lax
from jax.experimental import pallas as pl
from jax.experimental.pallas import tpu as pltpu
from jax.sharding import PartitionSpec as P

NSUB = 3
CAP = 8
HALO = 3
PAD_ROWS = 8
PAD_LANES = 128


def exact_dot(left, right, left_dim):
    return lax.dot_general(
        left,
        right,
        (((left_dim,), (0,)), ((), ())),
        precision=lax.Precision.HIGHEST,
        preferred_element_type=jnp.float32,
    )


def mix_kernel(adj_ref, mask_ref, diff_ref, rows_ref, cols_ref, cor_ref, out_ref, xs, ds):
    fields = adj_ref.shape[0]
    h, w = adj_ref.shape[2], adj_ref.shape[3]
    hp, wp = xs.shape[1], xs.shape[2]
    wet = mask_ref[0].astype(jnp.float32)
    for f in range(fields):
        xs[f, 0:h, 0:w] = adj_ref[f, 0] * wet
        xs[f, h:hp, 0:w] = rows_ref[f, 0]
        xs[f, :, w:wp] = cols_ref[f, 0]
    ds[0:h, 0:w] = diff_ref[0]
    ds[h:hp, 0:w] = rows_ref[fields, 0]
    ds[:, w:wp] = cols_ref[fields, 0]
    d = ds[...]
    done = []
    for f in range(fields):
        x = xs[f]
        for _ in range(NSUB):
            east = pltpu.roll(x, wp - 1, 1)
            west = pltpu.roll(x, 1, 1)
            north = pltpu.roll(x, hp - 1, 0)
            south = pltpu.roll(x, 1, 0)
            x = x + d * (east + west + north + south - 4.0 * x)
        done.append(x[0:h, 0:w])
    rot = cor_ref[...]
    out_ref[0, 0] = wet * done[0]
    out_ref[1, 0] = wet * done[1]
    out_ref[2, 0] = wet * (done[2] - rot * done[3])
    out_ref[3, 0] = wet * (done[3] + rot * done[2])


def mix_call(adjoint, land_mask, diffusivity, rows5, cols5, coriolis):
    fields, levels, h, w = adjoint.shape
    hp, wp = h + PAD_ROWS, w + PAD_LANES
    return pl.pallas_call(
        mix_kernel,
        grid=(levels,),
        in_specs=[
            pl.BlockSpec((fields, 1, h, w), lambda k: (0, k, 0, 0)),
            pl.BlockSpec((1, h, w), lambda k: (k, 0, 0)),
            pl.BlockSpec((1, h, w), lambda k: (k, 0, 0)),
            pl.BlockSpec((fields + 1, 1, PAD_ROWS, w), lambda k: (0, k, 0, 0)),
            pl.BlockSpec((fields + 1, 1, hp, PAD_LANES), lambda k: (0, k, 0, 0)),
            pl.BlockSpec((h, 1), lambda k: (0, 0)),
        ],
        out_specs=pl.BlockSpec((fields, 1, h, w), lambda k: (0, k, 0, 0)),
        out_shape=jax.ShapeDtypeStruct(adjoint.shape, jnp.float32),
        scratch_shapes=[
            pltpu.VMEM((fields, hp, wp), jnp.float32),
            pltpu.VMEM((hp, wp), jnp.float32),
        ],
    )(adjoint, land_mask, diffusivity, rows5, cols5, coriolis.reshape(h, 1))


def obs_kernel(where_ref, weight_ref, vals_ref, traj_ref, mask_ref, base_ref, out_ref):
    out_ref[...] = base_ref[...]
    seg_width = vals_ref.shape[1]
    sub = lax.broadcasted_iota(jnp.int32, (8, seg_width), 0)

    def body(o, carry):
        first = pl.multiple_of(o * 8, 8)
        vals8 = vals_ref[pl.ds(first, 8), :]
        for j in range(8):
            i = first + j

            @pl.when(weight_ref[i] != 0.0)
            def _():
                add_row(i, vals8[j : j + 1, :])

        return carry

    def add_row(i, value):
        layer = where_ref[0, i]
        row = where_ref[1, i]
        col = pl.multiple_of(where_ref[2, i], seg_width)
        level = where_ref[3, i]
        tile = pl.multiple_of((row // 8) * 8, 8)
        rows = pl.ds(tile, 8)
        cols = pl.ds(col, seg_width)
        sampled = traj_ref[layer, rows, cols]
        misfit = weight_ref[i] * (sampled - value)
        wet = mask_ref[level, rows, cols].astype(jnp.float32)
        hit = sub == row - tile
        cur = out_ref[layer, rows, cols]
        out_ref[layer, rows, cols] = cur + jnp.where(hit, wet * misfit, 0.0)

    lax.fori_loop(0, vals_ref.shape[0] // 8, body, 0)


def obs_call(where, weight, values, traj3, land_mask, base3):
    whole = lambda shape: pl.BlockSpec(shape, lambda i, *_: (0,) * len(shape))
    return pl.pallas_call(
        obs_kernel,
        grid_spec=pltpu.PrefetchScalarGridSpec(
            num_scalar_prefetch=2,
            grid=(1,),
            in_specs=[
                whole(values.shape),
                whole(traj3.shape),
                whole(land_mask.shape),
                whole(base3.shape),
            ],
            out_specs=whole(base3.shape),
        ),
        out_shape=jax.ShapeDtypeStruct(base3.shape, jnp.float32),
        compiler_params=pltpu.CompilerParams(vmem_limit_bytes=60 * 1024 * 1024),
    )(where, weight, values, traj3, land_mask, base3)


def fold_rows(top_msg, fold_partner, width):
    lon_count = lax.axis_size("lon")
    lat_count = lax.axis_size("lat")
    lon = lax.axis_index("lon")
    nx = lon_count * width
    first = lon * width
    offset = (fold_partner[0] + first - (nx - 1)) % nx
    shift_tiles = offset // width
    shift_in = offset % width
    top = lat_count - 1

    def branch(q):
        def run(msg):
            pairs_a, pairs_b = [], []
            for t in range(lon_count):
                src_a = (lon_count - 1 - t + q) % lon_count
                src_b = (src_a + 1) % lon_count
                pairs_a.append((src_a * lat_count + top, t * lat_count + top))
                pairs_b.append((src_b * lat_count + top, t * lat_count + top))
            got_a = lax.ppermute(msg, ("lon", "lat"), pairs_a)
            got_b = lax.ppermute(msg, ("lon", "lat"), pairs_b)
            return jnp.concatenate([got_a, got_b], axis=2)

        return run

    both = lax.switch(shift_tiles, [branch(q) for q in range(lon_count)], top_msg)
    source = lax.broadcasted_iota(jnp.int32, (2 * width, width), 0)
    target = lax.broadcasted_iota(jnp.int32, (2 * width, width), 1)
    pick = (source == width - 1 - target + shift_in).astype(jnp.float32)
    return exact_dot(both, pick, 2)


def per_device(
    adjoint,
    trajectory,
    diffusivity,
    land_mask,
    coriolis,
    obs_values,
    obs_weight,
    obs_owner,
    obs_offset,
    fold_partner,
):
    fields, levels, h, w = adjoint.shape
    lat_count = lax.axis_size("lat")
    lon_count = lax.axis_size("lon")
    lat = lax.axis_index("lat")
    n_work = fields * levels
    sign = jnp.array([1.0, 1.0, -1.0, -1.0], jnp.float32).reshape(fields, 1, 1, 1)

    def edge(rows):
        wet_rows = land_mask[:, rows, :].astype(jnp.float32)
        work_rows = adjoint[:, :, rows, :] * wet_rows[None]
        return work_rows, diffusivity[:, rows, :]

    top_work, top_diff = edge(slice(h - HALO, h))
    bot_work, bot_diff = edge(slice(0, HALO))
    top_msg = jnp.concatenate([top_work.reshape(n_work, HALO, w), top_diff], axis=0)
    bot_msg = jnp.concatenate([bot_work.reshape(n_work, HALO, w), bot_diff], axis=0)
    up = [(i, i + 1) for i in range(lat_count - 1)]
    down = [(i + 1, i) for i in range(lat_count - 1)]
    from_below = lax.ppermute(top_msg, "lat", up)
    from_above = lax.ppermute(bot_msg, "lat", down)
    signed_top = jnp.concatenate(
        [(top_work * sign).reshape(n_work, HALO, w), top_diff], axis=0
    )
    signed_top = jnp.concatenate(
        [signed_top[:, HALO - 1 - m : HALO - m, :] for m in range(HALO)], axis=1
    )
    folded = fold_rows(signed_top, fold_partner, w)
    north = jnp.where(lat == lat_count - 1, folded, from_above)
    gap = jnp.zeros((n_work + levels, PAD_ROWS - 2 * HALO, w), jnp.float32)
    rows_all = jnp.concatenate([north, gap, from_below], axis=1)
    rows5 = rows_all.reshape(fields + 1, levels, PAD_ROWS, w)

    work_first = adjoint[:, :, :, :HALO] * land_mask[None, :, :, :HALO].astype(jnp.float32)
    work_last = adjoint[:, :, :, w - HALO :] * land_mask[None, :, :, w - HALO :].astype(jnp.float32)
    first = jnp.concatenate(
        [
            jnp.concatenate([work_first.reshape(n_work, h, HALO), diffusivity[:, :, :HALO]], 0),
            rows_all[:, :, :HALO],
        ],
        axis=1,
    )
    last = jnp.concatenate(
        [
            jnp.concatenate([work_last.reshape(n_work, h, HALO), diffusivity[:, :, w - HALO :]], 0),
            rows_all[:, :, w - HALO :],
        ],
        axis=1,
    )
    ring_west = [(i, (i - 1) % lon_count) for i in range(lon_count)]
    ring_east = [(i, (i + 1) % lon_count) for i in range(lon_count)]
    first_t = jnp.swapaxes(first, 1, 2)
    last_t = jnp.swapaxes(last, 1, 2)
    east_halo = jnp.swapaxes(lax.ppermute(first_t, "lon", ring_west), 1, 2)
    west_halo = jnp.swapaxes(lax.ppermute(last_t, "lon", ring_east), 1, 2)
    hp = h + PAD_ROWS
    middle = jnp.zeros((n_work + levels, hp, PAD_LANES - 2 * HALO), jnp.float32)
    cols5 = jnp.concatenate([east_halo, middle, west_halo], axis=2).reshape(
        fields + 1, levels, hp, PAD_LANES
    )

    mixed_wet = mix_call(adjoint, land_mask, diffusivity, rows5, cols5, coriolis)

    devices = lon_count * lat_count
    seg_width = obs_values.shape[1]
    rows_sent = obs_values.shape[0]
    owner_index = obs_owner[:, 0]
    one_hot = (owner_index[:, None] == jnp.arange(devices, dtype=jnp.int32)[None, :]).astype(
        jnp.bfloat16
    )
    row_ids = jnp.arange(rows_sent, dtype=jnp.int32)
    before = (row_ids[None, :] < row_ids[:, None]).astype(jnp.bfloat16)
    earlier = lax.dot_general(
        before, one_hot, (((1,), (0,)), ((), ())), preferred_element_type=jnp.float32
    )
    slot_index = jnp.sum(earlier * one_hot.astype(jnp.float32), axis=1).astype(jnp.int32)
    dest_index = owner_index * CAP + slot_index
    slot_ids = jnp.arange(devices * CAP, dtype=jnp.int32)
    placement = (dest_index[:, None] == slot_ids[None, :]).astype(jnp.float32)
    send_values = exact_dot(placement, obs_values, 0).reshape(devices, CAP, seg_width)
    meta = jnp.stack([obs_weight, obs_offset.astype(jnp.float32)], axis=1)
    send_meta = exact_dot(placement, meta, 0).reshape(devices, CAP, 2)
    send_meta = jnp.swapaxes(send_meta, 1, 2).reshape(devices, 2 * CAP)
    send_meta = jnp.pad(send_meta, ((0, 0), (0, seg_width - 2 * CAP)))
    send = jnp.concatenate([send_values.reshape(devices, CAP * seg_width), send_meta], axis=1)
    got = lax.all_to_all(send, ("lon", "lat"), split_axis=0, concat_axis=0, tiled=True)
    got_values = got[:, : CAP * seg_width].reshape(devices * CAP, seg_width)
    got_meta = got[:, CAP * seg_width : CAP * seg_width + 2 * CAP].reshape(devices, 2, CAP)
    got_weight = got_meta[:, 0, :].reshape(devices * CAP)
    got_offset = got_meta[:, 1, :].reshape(devices * CAP).astype(jnp.int32)

    segments = w // seg_width
    seg_local = got_offset % segments
    rest = got_offset // segments
    row_local = rest % h
    layer = rest // h
    where = jnp.stack([layer, row_local, seg_local * seg_width, layer % levels], axis=0)
    out3 = obs_call(
        where,
        got_weight,
        got_values,
        trajectory.reshape(n_work, h, w),
        land_mask,
        mixed_wet.reshape(n_work, h, w),
    )
    return out3.reshape(adjoint.shape)


def solution(mesh):
    return jax.shard_map(
        per_device,
        mesh=mesh,
        in_specs=(
            P(None, None, "lat", "lon"),
            P(None, None, "lat", "lon"),
            P(None, "lat", "lon"),
            P(None, "lat", "lon"),
            P("lat"),
            P(("lon", "lat"), None),
            P(("lon", "lat")),
            P(("lon", "lat"), None),
            P(("lon", "lat")),
            P("lon"),
        ),
        out_specs=P(None, None, "lat", "lon"),
        check_vma=False,
    )
```

```python
import functools

import jax
import jax.numpy as jnp
from jax import lax
from jax.experimental import pallas as pl
from jax.experimental.pallas import tpu as pltpu
from jax.sharding import PartitionSpec as P

NSUB = 3
CAP = 8
HALO = 3
PAD_ROWS = 8
PAD_LANES = 128


def exact_dot(left, right, left_dim):
    return lax.dot_general(
        left,
        right,
        (((left_dim,), (0,)), ((), ())),
        precision=lax.Precision.HIGHEST,
        preferred_element_type=jnp.float32,
    )


def mix_kernel(adj_ref, mask_ref, diff_ref, rows_ref, cols_ref, cor_ref, out_ref, xs, ds):
    fields = adj_ref.shape[0]
    h, w = adj_ref.shape[2], adj_ref.shape[3]
    hp, wp = xs.shape[1], xs.shape[2]
    wet = mask_ref[0].astype(jnp.float32)
    for f in range(fields):
        xs[f, 0:h, 0:w] = adj_ref[f, 0] * wet
        xs[f, h:hp, 0:w] = rows_ref[f, 0]
        xs[f, :, w:wp] = cols_ref[f, 0]
    ds[0:h, 0:w] = diff_ref[0]
    ds[h:hp, 0:w] = rows_ref[fields, 0]
    ds[:, w:wp] = cols_ref[fields, 0]
    d = ds[...]
    done = []
    for f in range(fields):
        x = xs[f]
        for _ in range(NSUB):
            east = pltpu.roll(x, wp - 1, 1)
            west = pltpu.roll(x, 1, 1)
            north = pltpu.roll(x, hp - 1, 0)
            south = pltpu.roll(x, 1, 0)
            x = x + d * (east + west + north + south - 4.0 * x)
        done.append(x[0:h, 0:w])
    rot = cor_ref[...]
    out_ref[0, 0] = wet * done[0]
    out_ref[1, 0] = wet * done[1]
    out_ref[2, 0] = wet * (done[2] - rot * done[3])
    out_ref[3, 0] = wet * (done[3] + rot * done[2])


def mix_call(adjoint, land_mask, diffusivity, rows5, cols5, coriolis):
    fields, levels, h, w = adjoint.shape
    hp, wp = h + PAD_ROWS, w + PAD_LANES
    return pl.pallas_call(
        mix_kernel,
        grid=(levels,),
        in_specs=[
            pl.BlockSpec((fields, 1, h, w), lambda k: (0, k, 0, 0)),
            pl.BlockSpec((1, h, w), lambda k: (k, 0, 0)),
            pl.BlockSpec((1, h, w), lambda k: (k, 0, 0)),
            pl.BlockSpec((fields + 1, 1, PAD_ROWS, w), lambda k: (0, k, 0, 0)),
            pl.BlockSpec((fields + 1, 1, hp, PAD_LANES), lambda k: (0, k, 0, 0)),
            pl.BlockSpec((h, 1), lambda k: (0, 0)),
        ],
        out_specs=pl.BlockSpec((fields, 1, h, w), lambda k: (0, k, 0, 0)),
        out_shape=jax.ShapeDtypeStruct(adjoint.shape, jnp.float32),
        scratch_shapes=[
            pltpu.VMEM((fields, hp, wp), jnp.float32),
            pltpu.VMEM((hp, wp), jnp.float32),
        ],
    )(adjoint, land_mask, diffusivity, rows5, cols5, coriolis.reshape(h, 1))


def obs_kernel(where_ref, weight_ref, vals_ref, traj_ref, mask_ref, base_ref, out_ref):
    out_ref[...] = base_ref[...]
    seg_width = vals_ref.shape[1]
    sub = lax.broadcasted_iota(jnp.int32, (8, seg_width), 0)

    def body(o, carry):
        first = pl.multiple_of(o * 8, 8)
        vals8 = vals_ref[pl.ds(first, 8), :]
        for j in range(8):
            add_row(first + j, vals8[j : j + 1, :])
        return carry

    def add_row(i, value):
        layer = where_ref[0, i]
        rows = pl.ds(pl.multiple_of(where_ref[1, i], 8), 8)
        cols = pl.ds(pl.multiple_of(where_ref[2, i], seg_width), seg_width)
        level = where_ref[3, i]
        sampled = traj_ref[layer, rows, cols]
        misfit = weight_ref[i] * (sampled - value)
        wet = mask_ref[level, rows, cols].astype(jnp.float32)
        hit = sub == where_ref[4, i]
        cur = out_ref[layer, rows, cols]
        out_ref[layer, rows, cols] = cur + jnp.where(hit, wet * misfit, 0.0)

    lax.fori_loop(0, vals_ref.shape[0] // 8, body, 0)


def obs_call(where, weight, values, traj3, land_mask, base3):
    whole = lambda shape: pl.BlockSpec(shape, lambda i, *_: (0,) * len(shape))
    return pl.pallas_call(
        obs_kernel,
        grid_spec=pltpu.PrefetchScalarGridSpec(
            num_scalar_prefetch=2,
            grid=(1,),
            in_specs=[
                whole(values.shape),
                whole(traj3.shape),
                whole(land_mask.shape),
                whole(base3.shape),
            ],
            out_specs=whole(base3.shape),
        ),
        out_shape=jax.ShapeDtypeStruct(base3.shape, jnp.float32),
        compiler_params=pltpu.CompilerParams(vmem_limit_bytes=60 * 1024 * 1024),
    )(where, weight, values, traj3, land_mask, base3)


def fold_rows(top_msg, fold_partner, width):
    lon_count = lax.axis_size("lon")
    lat_count = lax.axis_size("lat")
    lon = lax.axis_index("lon")
    nx = lon_count * width
    first = lon * width
    offset = (fold_partner[0] + first - (nx - 1)) % nx
    shift_tiles = offset // width
    shift_in = offset % width
    top = lat_count - 1

    def branch(q):
        def run(msg):
            pairs_a, pairs_b = [], []
            for t in range(lon_count):
                src_a = (lon_count - 1 - t + q) % lon_count
                src_b = (src_a + 1) % lon_count
                pairs_a.append((src_a * lat_count + top, t * lat_count + top))
                pairs_b.append((src_b * lat_count + top, t * lat_count + top))
            got_a = lax.ppermute(msg, ("lon", "lat"), pairs_a)
            got_b = lax.ppermute(msg, ("lon", "lat"), pairs_b)
            return jnp.concatenate([got_a, got_b], axis=2)

        return run

    both = lax.switch(shift_tiles, [branch(q) for q in range(lon_count)], top_msg)
    source = lax.broadcasted_iota(jnp.int32, (2 * width, width), 0)
    target = lax.broadcasted_iota(jnp.int32, (2 * width, width), 1)
    pick = (source == width - 1 - target + shift_in).astype(jnp.float32)
    return exact_dot(both, pick, 2)


def per_device(
    adjoint,
    trajectory,
    diffusivity,
    land_mask,
    coriolis,
    obs_values,
    obs_weight,
    obs_owner,
    obs_offset,
    fold_partner,
):
    fields, levels, h, w = adjoint.shape
    lat_count = lax.axis_size("lat")
    lon_count = lax.axis_size("lon")
    lat = lax.axis_index("lat")
    n_work = fields * levels
    sign = jnp.array([1.0, 1.0, -1.0, -1.0], jnp.float32).reshape(fields, 1, 1, 1)

    def edge(rows):
        wet_rows = land_mask[:, rows, :].astype(jnp.float32)
        work_rows = adjoint[:, :, rows, :] * wet_rows[None]
        return work_rows, diffusivity[:, rows, :]

    top_work, top_diff = edge(slice(h - HALO, h))
    bot_work, bot_diff = edge(slice(0, HALO))
    top_msg = jnp.concatenate([top_work.reshape(n_work, HALO, w), top_diff], axis=0)
    bot_msg = jnp.concatenate([bot_work.reshape(n_work, HALO, w), bot_diff], axis=0)
    up = [(i, i + 1) for i in range(lat_count - 1)]
    down = [(i + 1, i) for i in range(lat_count - 1)]
    from_below = lax.ppermute(top_msg, "lat", up)
    from_above = lax.ppermute(bot_msg, "lat", down)
    signed_top = jnp.concatenate(
        [(top_work * sign).reshape(n_work, HALO, w), top_diff], axis=0
    )
    signed_top = jnp.concatenate(
        [signed_top[:, HALO - 1 - m : HALO - m, :] for m in range(HALO)], axis=1
    )
    folded = fold_rows(signed_top, fold_partner, w)
    north = jnp.where(lat == lat_count - 1, folded, from_above)
    gap = jnp.zeros((n_work + levels, PAD_ROWS - 2 * HALO, w), jnp.float32)
    rows_all = jnp.concatenate([north, gap, from_below], axis=1)
    rows5 = rows_all.reshape(fields + 1, levels, PAD_ROWS, w)

    work_first = adjoint[:, :, :, :HALO] * land_mask[None, :, :, :HALO].astype(jnp.float32)
    work_last = adjoint[:, :, :, w - HALO :] * land_mask[None, :, :, w - HALO :].astype(jnp.float32)
    first = jnp.concatenate(
        [
            jnp.concatenate([work_first.reshape(n_work, h, HALO), diffusivity[:, :, :HALO]], 0),
            rows_all[:, :, :HALO],
        ],
        axis=1,
    )
    last = jnp.concatenate(
        [
            jnp.concatenate([work_last.reshape(n_work, h, HALO), diffusivity[:, :, w - HALO :]], 0),
            rows_all[:, :, w - HALO :],
        ],
        axis=1,
    )
    ring_west = [(i, (i - 1) % lon_count) for i in range(lon_count)]
    ring_east = [(i, (i + 1) % lon_count) for i in range(lon_count)]
    first_t = jnp.swapaxes(first, 1, 2)
    last_t = jnp.swapaxes(last, 1, 2)
    east_halo = jnp.swapaxes(lax.ppermute(first_t, "lon", ring_west), 1, 2)
    west_halo = jnp.swapaxes(lax.ppermute(last_t, "lon", ring_east), 1, 2)
    hp = h + PAD_ROWS
    middle = jnp.zeros((n_work + levels, hp, PAD_LANES - 2 * HALO), jnp.float32)
    cols5 = jnp.concatenate([east_halo, middle, west_halo], axis=2).reshape(
        fields + 1, levels, hp, PAD_LANES
    )

    mixed_wet = mix_call(adjoint, land_mask, diffusivity, rows5, cols5, coriolis)

    devices = lon_count * lat_count
    seg_width = obs_values.shape[1]
    rows_sent = obs_values.shape[0]
    owner_index = obs_owner[:, 0]
    one_hot = (owner_index[:, None] == jnp.arange(devices, dtype=jnp.int32)[None, :]).astype(
        jnp.bfloat16
    )
    row_ids = jnp.arange(rows_sent, dtype=jnp.int32)
    before = (row_ids[None, :] < row_ids[:, None]).astype(jnp.bfloat16)
    earlier = lax.dot_general(
        before, one_hot, (((1,), (0,)), ((), ())), preferred_element_type=jnp.float32
    )
    slot_index = jnp.sum(earlier * one_hot.astype(jnp.float32), axis=1).astype(jnp.int32)
    dest_index = owner_index * CAP + slot_index
    slot_ids = jnp.arange(devices * CAP, dtype=jnp.int32)
    placement = (dest_index[:, None] == slot_ids[None, :]).astype(jnp.float32)
    send_values = exact_dot(placement, obs_values, 0).reshape(devices, CAP, seg_width)
    meta = jnp.stack([obs_weight, obs_offset.astype(jnp.float32)], axis=1)
    send_meta = exact_dot(placement, meta, 0).reshape(devices, CAP, 2)
    send_meta = jnp.swapaxes(send_meta, 1, 2).reshape(devices, 2 * CAP)
    send_meta = jnp.pad(send_meta, ((0, 0), (0, seg_width - 2 * CAP)))
    send = jnp.concatenate([send_values.reshape(devices, CAP * seg_width), send_meta], axis=1)
    send = send.reshape(lon_count, lat_count, send.shape[1])
    hop = lax.all_to_all(send, "lat", split_axis=1, concat_axis=1, tiled=True)
    got = lax.all_to_all(hop, "lon", split_axis=0, concat_axis=0, tiled=True)
    got = got.reshape(devices, got.shape[2])
    got_values = got[:, : CAP * seg_width].reshape(devices * CAP, seg_width)
    got_meta = got[:, CAP * seg_width : CAP * seg_width + 2 * CAP].reshape(devices, 2, CAP)
    got_weight = got_meta[:, 0, :].reshape(devices * CAP)
    got_offset = got_meta[:, 1, :].reshape(devices * CAP).astype(jnp.int32)

    segments = w // seg_width
    seg_local = got_offset % segments
    rest = got_offset // segments
    row_local = rest % h
    layer = rest // h
    where = jnp.stack(
        [layer, row_local // 8 * 8, seg_local * seg_width, layer % levels, row_local % 8], axis=0
    )
    out3 = obs_call(
        where,
        got_weight,
        got_values,
        trajectory.reshape(n_work, h, w),
        land_mask,
        mixed_wet.reshape(n_work, h, w),
    )
    return out3.reshape(adjoint.shape)


def solution(mesh):
    return jax.shard_map(
        per_device,
        mesh=mesh,
        in_specs=(
            P(None, None, "lat", "lon"),
            P(None, None, "lat", "lon"),
            P(None, "lat", "lon"),
            P(None, "lat", "lon"),
            P("lat"),
            P(("lon", "lat"), None),
            P(("lon", "lat")),
            P(("lon", "lat"), None),
            P(("lon", "lat")),
            P("lon"),
        ),
        out_specs=P(None, None, "lat", "lon"),
        check_vma=False,
    )
```

```python
import functools

import jax
import jax.numpy as jnp
from jax import lax
from jax.experimental import pallas as pl
from jax.experimental.pallas import tpu as pltpu
from jax.sharding import PartitionSpec as P

NSUB = 3
CAP = 8
HALO = 3
PAD_ROWS = 8
PAD_LANES = 128


def exact_dot(left, right, left_dim):
    return lax.dot_general(
        left,
        right,
        (((left_dim,), (0,)), ((), ())),
        precision=lax.Precision.HIGHEST,
        preferred_element_type=jnp.float32,
    )


def mix_kernel(adj_ref, mask_ref, diff_ref, rows_ref, cols_ref, cor_ref, out_ref, xs, ds):
    fields = adj_ref.shape[0]
    h, w = adj_ref.shape[2], adj_ref.shape[3]
    hp, wp = xs.shape[1], xs.shape[2]
    wet = mask_ref[0].astype(jnp.float32)
    for f in range(fields):
        xs[f, 0:h, 0:w] = adj_ref[f, 0] * wet
        xs[f, h:hp, 0:w] = rows_ref[f, 0]
        xs[f, :, w:wp] = cols_ref[f, 0]
    ds[0:h, 0:w] = diff_ref[0]
    ds[h:hp, 0:w] = rows_ref[fields, 0]
    ds[:, w:wp] = cols_ref[fields, 0]
    d = ds[...]
    done = []
    for f in range(fields):
        x = xs[f]
        for _ in range(NSUB):
            east = pltpu.roll(x, wp - 1, 1)
            west = pltpu.roll(x, 1, 1)
            north = pltpu.roll(x, hp - 1, 0)
            south = pltpu.roll(x, 1, 0)
            x = x + d * (east + west + north + south - 4.0 * x)
        done.append(x[0:h, 0:w])
    rot = cor_ref[...]
    out_ref[0, 0] = wet * done[0]
    out_ref[1, 0] = wet * done[1]
    out_ref[2, 0] = wet * (done[2] - rot * done[3])
    out_ref[3, 0] = wet * (done[3] + rot * done[2])


def mix_call(adjoint, land_mask, diffusivity, rows5, cols5, coriolis):
    fields, levels, h, w = adjoint.shape
    hp, wp = h + PAD_ROWS, w + PAD_LANES
    return pl.pallas_call(
        mix_kernel,
        grid=(levels,),
        in_specs=[
            pl.BlockSpec((fields, 1, h, w), lambda k: (0, k, 0, 0)),
            pl.BlockSpec((1, h, w), lambda k: (k, 0, 0)),
            pl.BlockSpec((1, h, w), lambda k: (k, 0, 0)),
            pl.BlockSpec((fields + 1, 1, PAD_ROWS, w), lambda k: (0, k, 0, 0)),
            pl.BlockSpec((fields + 1, 1, hp, PAD_LANES), lambda k: (0, k, 0, 0)),
            pl.BlockSpec((h, 1), lambda k: (0, 0)),
        ],
        out_specs=pl.BlockSpec((fields, 1, h, w), lambda k: (0, k, 0, 0)),
        out_shape=jax.ShapeDtypeStruct(adjoint.shape, jnp.float32),
        scratch_shapes=[
            pltpu.VMEM((fields, hp, wp), jnp.float32),
            pltpu.VMEM((hp, wp), jnp.float32),
        ],
    )(adjoint, land_mask, diffusivity, rows5, cols5, coriolis.reshape(h, 1))


def obs_kernel(where_ref, weight_ref, vals_ref, traj_ref, mask_ref, base_ref, out_ref):
    out_ref[...] = base_ref[...]
    seg_width = vals_ref.shape[1]
    sub = lax.broadcasted_iota(jnp.int32, (8, seg_width), 0)

    def body(o, carry):
        first = pl.multiple_of(o * 8, 8)
        vals8 = vals_ref[pl.ds(first, 8), :]
        for j in range(8):
            add_row(first + j, vals8[j : j + 1, :])
        return carry

    def add_row(i, value):
        layer = where_ref[0, i]
        rows = pl.ds(pl.multiple_of(where_ref[1, i], 8), 8)
        cols = pl.ds(pl.multiple_of(where_ref[2, i], seg_width), seg_width)
        level = where_ref[3, i]
        sampled = traj_ref[layer, rows, cols]
        misfit = weight_ref[i] * (sampled - value)
        wet = mask_ref[level, rows, cols].astype(jnp.float32)
        hit = sub == where_ref[4, i]
        cur = out_ref[layer, rows, cols]
        out_ref[layer, rows, cols] = cur + jnp.where(hit, wet * misfit, 0.0)

    lax.fori_loop(0, vals_ref.shape[0] // 8, body, 0)


def obs_call(where, weight, values, traj3, land_mask, base3):
    whole = lambda shape: pl.BlockSpec(shape, lambda i, *_: (0,) * len(shape))
    return pl.pallas_call(
        obs_kernel,
        grid_spec=pltpu.PrefetchScalarGridSpec(
            num_scalar_prefetch=2,
            grid=(1,),
            in_specs=[
                whole(values.shape),
                whole(traj3.shape),
                whole(land_mask.shape),
                whole(base3.shape),
            ],
            out_specs=whole(base3.shape),
        ),
        out_shape=jax.ShapeDtypeStruct(base3.shape, jnp.float32),
        compiler_params=pltpu.CompilerParams(vmem_limit_bytes=60 * 1024 * 1024),
    )(where, weight, values, traj3, land_mask, base3)


def fold_rows(top_msg, fold_partner, width):
    lon_count = lax.axis_size("lon")
    lat_count = lax.axis_size("lat")
    lon = lax.axis_index("lon")
    nx = lon_count * width
    first = lon * width
    offset = (fold_partner[0] + first - (nx - 1)) % nx
    shift_tiles = offset // width
    shift_in = offset % width
    top = lat_count - 1

    def branch(q):
        def run(msg):
            pairs_a, pairs_b = [], []
            for t in range(lon_count):
                src_a = (lon_count - 1 - t + q) % lon_count
                src_b = (src_a + 1) % lon_count
                pairs_a.append((src_a * lat_count + top, t * lat_count + top))
                pairs_b.append((src_b * lat_count + top, t * lat_count + top))
            got_a = lax.ppermute(msg, ("lon", "lat"), pairs_a)
            got_b = lax.ppermute(msg, ("lon", "lat"), pairs_b)
            return jnp.concatenate([got_a, got_b], axis=2)

        return run

    both = lax.switch(shift_tiles, [branch(q) for q in range(lon_count)], top_msg)
    source = lax.broadcasted_iota(jnp.int32, (2 * width, width), 0)
    target = lax.broadcasted_iota(jnp.int32, (2 * width, width), 1)
    pick = (source == width - 1 - target + shift_in).astype(jnp.float32)
    return exact_dot(both, pick, 2)


def per_device(
    adjoint,
    trajectory,
    diffusivity,
    land_mask,
    coriolis,
    obs_values,
    obs_weight,
    obs_owner,
    obs_offset,
    fold_partner,
):
    fields, levels, h, w = adjoint.shape
    lat_count = lax.axis_size("lat")
    lon_count = lax.axis_size("lon")
    lat = lax.axis_index("lat")
    n_work = fields * levels
    sign = jnp.array([1.0, 1.0, -1.0, -1.0], jnp.float32).reshape(fields, 1, 1, 1)

    def edge(rows):
        wet_rows = land_mask[:, rows, :].astype(jnp.float32)
        work_rows = adjoint[:, :, rows, :] * wet_rows[None]
        return work_rows, diffusivity[:, rows, :]

    top_work, top_diff = edge(slice(h - HALO, h))
    bot_work, bot_diff = edge(slice(0, HALO))
    top_msg = jnp.concatenate([top_work.reshape(n_work, HALO, w), top_diff], axis=0)
    bot_msg = jnp.concatenate([bot_work.reshape(n_work, HALO, w), bot_diff], axis=0)
    up = [(i, i + 1) for i in range(lat_count - 1)]
    down = [(i + 1, i) for i in range(lat_count - 1)]
    from_below = lax.ppermute(top_msg, "lat", up)
    from_above = lax.ppermute(bot_msg, "lat", down)
    signed_top = jnp.concatenate(
        [(top_work * sign).reshape(n_work, HALO, w), top_diff], axis=0
    )
    signed_top = jnp.concatenate(
        [signed_top[:, HALO - 1 - m : HALO - m, :] for m in range(HALO)], axis=1
    )
    folded = fold_rows(signed_top, fold_partner, w)
    north = jnp.where(lat == lat_count - 1, folded, from_above)
    gap = jnp.zeros((n_work + levels, PAD_ROWS - 2 * HALO, w), jnp.float32)
    rows_all = jnp.concatenate([north, gap, from_below], axis=1)
    rows5 = rows_all.reshape(fields + 1, levels, PAD_ROWS, w)

    lane = lax.broadcasted_iota(jnp.int32, (PAD_LANES, PAD_ROWS), 0)
    slot = lax.broadcasted_iota(jnp.int32, (PAD_LANES, PAD_ROWS), 1)
    take_first = (slot < HALO) & (lane == slot)
    take_last = (slot >= PAD_ROWS - HALO) & (lane == slot + PAD_LANES - PAD_ROWS)

    def edges(block):
        pick = lambda part, sel: jnp.einsum(
            "nyx,xc->ncy", part, sel.astype(jnp.float32), precision=lax.Precision.HIGHEST
        )
        return pick(block[..., :PAD_LANES], take_first) + pick(block[..., w - PAD_LANES :], take_last)

    wet_edges = edges(land_mask.astype(jnp.float32))
    adj_edges = edges(adjoint.reshape(n_work, h, w)).reshape(fields, levels, PAD_ROWS, h)
    work_edges = (adj_edges * wet_edges[None]).reshape(n_work, PAD_ROWS, h)
    interior = jnp.concatenate([work_edges, edges(diffusivity)], axis=0)
    col_msg = jnp.concatenate([interior, edges(rows_all)], axis=2)
    ring_west = [(i, (i - 1) % lon_count) for i in range(lon_count)]
    ring_east = [(i, (i + 1) % lon_count) for i in range(lon_count)]
    from_east = lax.ppermute(col_msg, "lon", ring_west)
    from_west = lax.ppermute(col_msg, "lon", ring_east)
    halo_slot = lax.broadcasted_iota(jnp.int32, col_msg.shape, 1)
    got_cols = jnp.where(halo_slot < HALO, from_east, from_west)
    place = (take_first | take_last).astype(jnp.float32).T
    cols5 = jnp.einsum("ncy,cl->nyl", got_cols, place, precision=lax.Precision.HIGHEST)
    cols5 = cols5.reshape(fields + 1, levels, h + PAD_ROWS, PAD_LANES)

    mixed_wet = mix_call(adjoint, land_mask, diffusivity, rows5, cols5, coriolis)

    devices = lon_count * lat_count
    seg_width = obs_values.shape[1]
    rows_sent = obs_values.shape[0]
    owner_index = obs_owner[:, 0]
    one_hot = (owner_index[:, None] == jnp.arange(devices, dtype=jnp.int32)[None, :]).astype(
        jnp.bfloat16
    )
    row_ids = jnp.arange(rows_sent, dtype=jnp.int32)
    before = (row_ids[None, :] < row_ids[:, None]).astype(jnp.bfloat16)
    earlier = lax.dot_general(
        before, one_hot, (((1,), (0,)), ((), ())), preferred_element_type=jnp.float32
    )
    slot_index = jnp.sum(earlier * one_hot.astype(jnp.float32), axis=1).astype(jnp.int32)
    dest_index = owner_index * CAP + slot_index
    slot_ids = jnp.arange(devices * CAP, dtype=jnp.int32)
    placement = (dest_index[:, None] == slot_ids[None, :]).astype(jnp.float32)
    send_values = exact_dot(placement, obs_values, 0).reshape(devices, CAP, seg_width)
    meta = jnp.stack([obs_weight, obs_offset.astype(jnp.float32)], axis=1)
    send_meta = exact_dot(placement, meta, 0).reshape(devices, CAP, 2)
    send_meta = jnp.swapaxes(send_meta, 1, 2).reshape(devices, 2 * CAP)
    send_meta = jnp.pad(send_meta, ((0, 0), (0, seg_width - 2 * CAP)))
    send = jnp.concatenate([send_values.reshape(devices, CAP * seg_width), send_meta], axis=1)
    got = lax.all_to_all(send, ("lon", "lat"), split_axis=0, concat_axis=0, tiled=True)
    got_values = got[:, : CAP * seg_width].reshape(devices * CAP, seg_width)
    got_meta = got[:, CAP * seg_width : CAP * seg_width + 2 * CAP].reshape(devices, 2, CAP)
    got_weight = got_meta[:, 0, :].reshape(devices * CAP)
    got_offset = got_meta[:, 1, :].reshape(devices * CAP).astype(jnp.int32)

    segments = w // seg_width
    seg_local = got_offset % segments
    rest = got_offset // segments
    row_local = rest % h
    layer = rest // h
    where = jnp.stack(
        [layer, row_local // 8 * 8, seg_local * seg_width, layer % levels, row_local % 8], axis=0
    )
    out3 = obs_call(
        where,
        got_weight,
        got_values,
        trajectory.reshape(n_work, h, w),
        land_mask,
        mixed_wet.reshape(n_work, h, w),
    )
    return out3.reshape(adjoint.shape)


def solution(mesh):
    return jax.shard_map(
        per_device,
        mesh=mesh,
        in_specs=(
            P(None, None, "lat", "lon"),
            P(None, None, "lat", "lon"),
            P(None, "lat", "lon"),
            P(None, "lat", "lon"),
            P("lat"),
            P(("lon", "lat"), None),
            P(("lon", "lat")),
            P(("lon", "lat"), None),
            P(("lon", "lat")),
            P("lon"),
        ),
        out_specs=P(None, None, "lat", "lon"),
        check_vma=False,
    )
```

```python
import jax
import jax.numpy as jnp
from jax import lax
from jax.experimental import pallas as pl
from jax.experimental.pallas import tpu as pltpu
from jax.sharding import PartitionSpec as P

NSUB = 3
CAP = 8
HALO = 3
PAD_ROWS = 8
PAD_LANES = 128


def exact_dot(left, right, left_dim):
    return lax.dot_general(
        left,
        right,
        (((left_dim,), (0,)), ((), ())),
        precision=lax.Precision.HIGHEST,
        preferred_element_type=jnp.float32,
    )


def step_kernel(
    where_ref, weight_ref, adj_ref, mask_ref, diff_ref, rows_ref, cols_ref, cor_ref, vals_ref,
    traj_hbm, out_ref, xs, ds, traj_ref, sem
):
    fields = adj_ref.shape[0]
    h, w = adj_ref.shape[2], adj_ref.shape[3]
    hp, wp = xs.shape[1], xs.shape[2]
    k = pl.program_id(0)
    last = pl.num_programs(0) - 1

    @pl.when(k == 0)
    def _():
        pltpu.make_async_copy(traj_hbm, traj_ref, sem).start()

    wet = mask_ref[k].astype(jnp.float32)
    for f in range(fields):
        xs[f, 0:h, 0:w] = adj_ref[f, 0] * wet
        xs[f, h:hp, 0:w] = rows_ref[f, 0]
        xs[f, :, w:wp] = cols_ref[f, 0]
    ds[0:h, 0:w] = diff_ref[0]
    ds[h:hp, 0:w] = rows_ref[fields, 0]
    ds[:, w:wp] = cols_ref[fields, 0]
    d = ds[...]
    done = []
    for f in range(fields):
        x = xs[f]
        for _ in range(NSUB):
            east = pltpu.roll(x, wp - 1, 1)
            west = pltpu.roll(x, 1, 1)
            north = pltpu.roll(x, hp - 1, 0)
            south = pltpu.roll(x, 1, 0)
            x = x + d * (east + west + north + south - 4.0 * x)
        done.append(x[0:h, 0:w])
    rot = cor_ref[...]
    out_ref[0, k] = wet * done[0]
    out_ref[1, k] = wet * done[1]
    out_ref[2, k] = wet * (done[2] - rot * done[3])
    out_ref[3, k] = wet * (done[3] + rot * done[2])

    @pl.when(k == last)
    def _():
        pltpu.make_async_copy(traj_hbm, traj_ref, sem).wait()
        add_forcing(where_ref, weight_ref, vals_ref, traj_ref, mask_ref, out_ref)


def add_forcing(where_ref, weight_ref, vals_ref, traj_ref, mask_ref, out_ref):
    seg_width = vals_ref.shape[1]
    sub = lax.broadcasted_iota(jnp.int32, (8, seg_width), 0)

    def add_row(i, value):
        layer = where_ref[0, i]
        rows = pl.ds(pl.multiple_of(where_ref[1, i], 8), 8)
        cols = pl.ds(pl.multiple_of(where_ref[2, i], seg_width), seg_width)
        level = where_ref[3, i]
        field = where_ref[5, i]
        sampled = traj_ref[layer, rows, cols]
        misfit = weight_ref[i] * (sampled - value)
        wet = mask_ref[level, rows, cols].astype(jnp.float32)
        hit = sub == where_ref[4, i]
        cur = out_ref[field, level, rows, cols]
        out_ref[field, level, rows, cols] = cur + jnp.where(hit, wet * misfit, 0.0)

    def body(o, carry):
        first = pl.multiple_of(o * 8, 8)
        vals8 = vals_ref[pl.ds(first, 8), :]
        for j in range(8):
            add_row(first + j, vals8[j : j + 1, :])
        return carry

    lax.fori_loop(0, vals_ref.shape[0] // 8, body, 0)


def step_call(where, weight, adjoint, land_mask, diffusivity, rows5, cols5, coriolis, values, traj3):
    fields, levels, h, w = adjoint.shape
    hp, wp = h + PAD_ROWS, w + PAD_LANES
    whole = lambda shape: pl.BlockSpec(shape, lambda k, *_: (0,) * len(shape))
    return pl.pallas_call(
        step_kernel,
        grid_spec=pltpu.PrefetchScalarGridSpec(
            num_scalar_prefetch=2,
            grid=(levels,),
            in_specs=[
                pl.BlockSpec((fields, 1, h, w), lambda k, *_: (0, k, 0, 0)),
                whole(land_mask.shape),
                pl.BlockSpec((1, h, w), lambda k, *_: (k, 0, 0)),
                pl.BlockSpec((fields + 1, 1, PAD_ROWS, w), lambda k, *_: (0, k, 0, 0)),
                pl.BlockSpec((fields + 1, 1, hp, PAD_LANES), lambda k, *_: (0, k, 0, 0)),
                whole((h, 1)),
                whole(values.shape),
                pl.BlockSpec(memory_space=pl.ANY),
            ],
            out_specs=whole(adjoint.shape),
            scratch_shapes=[
                pltpu.VMEM((fields, hp, wp), jnp.float32),
                pltpu.VMEM((hp, wp), jnp.float32),
                pltpu.VMEM(traj3.shape, jnp.float32),
                pltpu.SemaphoreType.DMA(()),
            ],
        ),
        out_shape=jax.ShapeDtypeStruct(adjoint.shape, jnp.float32),
        compiler_params=pltpu.CompilerParams(vmem_limit_bytes=60 * 1024 * 1024),
    )(where, weight, adjoint, land_mask, diffusivity, rows5, cols5, coriolis.reshape(h, 1), values, traj3)


def fold_rows(top_msg, fold_partner, width):
    lon_count = lax.axis_size("lon")
    lat_count = lax.axis_size("lat")
    lon = lax.axis_index("lon")
    nx = lon_count * width
    first = lon * width
    offset = (fold_partner[0] + first - (nx - 1)) % nx
    shift_tiles = offset // width
    shift_in = offset % width
    top = lat_count - 1

    def branch(q):
        def run(msg):
            pairs_a, pairs_b = [], []
            for t in range(lon_count):
                src_a = (lon_count - 1 - t + q) % lon_count
                src_b = (src_a + 1) % lon_count
                pairs_a.append((src_a * lat_count + top, t * lat_count + top))
                pairs_b.append((src_b * lat_count + top, t * lat_count + top))
            got_a = lax.ppermute(msg, ("lon", "lat"), pairs_a)
            got_b = lax.ppermute(msg, ("lon", "lat"), pairs_b)
            return jnp.concatenate([got_a, got_b], axis=2)

        return run

    both = lax.switch(shift_tiles, [branch(q) for q in range(lon_count)], top_msg)
    source = lax.broadcasted_iota(jnp.int32, (2 * width, width), 0)
    target = lax.broadcasted_iota(jnp.int32, (2 * width, width), 1)
    pick = (source == width - 1 - target + shift_in).astype(jnp.float32)
    return exact_dot(both, pick, 2)


def per_device(
    adjoint,
    trajectory,
    diffusivity,
    land_mask,
    coriolis,
    obs_values,
    obs_weight,
    obs_owner,
    obs_offset,
    fold_partner,
):
    fields, levels, h, w = adjoint.shape
    lat_count = lax.axis_size("lat")
    lon_count = lax.axis_size("lon")
    lat = lax.axis_index("lat")
    n_work = fields * levels
    sign = jnp.array([1.0, 1.0, -1.0, -1.0], jnp.float32).reshape(fields, 1, 1, 1)

    def edge(rows):
        wet_rows = land_mask[:, rows, :].astype(jnp.float32)
        work_rows = adjoint[:, :, rows, :] * wet_rows[None]
        return work_rows, diffusivity[:, rows, :]

    top_work, top_diff = edge(slice(h - HALO, h))
    bot_work, bot_diff = edge(slice(0, HALO))
    top_msg = jnp.concatenate([top_work.reshape(n_work, HALO, w), top_diff], axis=0)
    bot_msg = jnp.concatenate([bot_work.reshape(n_work, HALO, w), bot_diff], axis=0)
    up = [(i, i + 1) for i in range(lat_count - 1)]
    down = [(i + 1, i) for i in range(lat_count - 1)]
    from_below = lax.ppermute(top_msg, "lat", up)
    from_above = lax.ppermute(bot_msg, "lat", down)
    signed_top = jnp.concatenate(
        [(top_work * sign).reshape(n_work, HALO, w), top_diff], axis=0
    )
    signed_top = jnp.concatenate(
        [signed_top[:, HALO - 1 - m : HALO - m, :] for m in range(HALO)], axis=1
    )
    folded = fold_rows(signed_top, fold_partner, w)
    north = jnp.where(lat == lat_count - 1, folded, from_above)
    gap = jnp.zeros((n_work + levels, PAD_ROWS - 2 * HALO, w), jnp.float32)
    rows_all = jnp.concatenate([north, gap, from_below], axis=1)
    rows5 = rows_all.reshape(fields + 1, levels, PAD_ROWS, w)

    lane = lax.broadcasted_iota(jnp.int32, (PAD_LANES, PAD_ROWS), 0)
    slot = lax.broadcasted_iota(jnp.int32, (PAD_LANES, PAD_ROWS), 1)
    take_first = (slot < HALO) & (lane == slot)
    take_last = (slot >= PAD_ROWS - HALO) & (lane == slot + PAD_LANES - PAD_ROWS)

    def edges(block):
        pick = lambda part, sel: jnp.einsum(
            "nyx,xc->ncy", part, sel.astype(jnp.float32), precision=lax.Precision.HIGHEST
        )
        return pick(block[..., :PAD_LANES], take_first) + pick(block[..., w - PAD_LANES :], take_last)

    wet_edges = edges(land_mask.astype(jnp.float32))
    adj_edges = edges(adjoint.reshape(n_work, h, w)).reshape(fields, levels, PAD_ROWS, h)
    work_edges = (adj_edges * wet_edges[None]).reshape(n_work, PAD_ROWS, h)
    interior = jnp.concatenate([work_edges, edges(diffusivity)], axis=0)
    col_msg = jnp.concatenate([interior, edges(rows_all)], axis=2)
    ring_west = [(i, (i - 1) % lon_count) for i in range(lon_count)]
    ring_east = [(i, (i + 1) % lon_count) for i in range(lon_count)]
    from_east = lax.ppermute(col_msg, "lon", ring_west)
    from_west = lax.ppermute(col_msg, "lon", ring_east)
    halo_slot = lax.broadcasted_iota(jnp.int32, col_msg.shape, 1)
    got_cols = jnp.where(halo_slot < HALO, from_east, from_west)
    place = (take_first | take_last).astype(jnp.float32).T
    cols5 = jnp.einsum("ncy,cl->nyl", got_cols, place, precision=lax.Precision.HIGHEST)
    cols5 = cols5.reshape(fields + 1, levels, h + PAD_ROWS, PAD_LANES)


    devices = lon_count * lat_count
    seg_width = obs_values.shape[1]
    rows_sent = obs_values.shape[0]
    owner_index = obs_owner[:, 0]
    one_hot = (owner_index[:, None] == jnp.arange(devices, dtype=jnp.int32)[None, :]).astype(
        jnp.bfloat16
    )
    row_ids = jnp.arange(rows_sent, dtype=jnp.int32)
    before = (row_ids[None, :] < row_ids[:, None]).astype(jnp.bfloat16)
    earlier = lax.dot_general(
        before, one_hot, (((1,), (0,)), ((), ())), preferred_element_type=jnp.float32
    )
    slot_index = jnp.sum(earlier * one_hot.astype(jnp.float32), axis=1).astype(jnp.int32)
    dest_index = owner_index * CAP + slot_index
    slot_ids = jnp.arange(devices * CAP, dtype=jnp.int32)
    placement = (dest_index[:, None] == slot_ids[None, :]).astype(jnp.float32)
    send_values = exact_dot(placement, obs_values, 0).reshape(devices, CAP, seg_width)
    meta = jnp.stack([obs_weight, obs_offset.astype(jnp.float32)], axis=1)
    send_meta = exact_dot(placement, meta, 0).reshape(devices, CAP, 2)
    send_meta = jnp.swapaxes(send_meta, 1, 2).reshape(devices, 2 * CAP)
    send_meta = jnp.pad(send_meta, ((0, 0), (0, seg_width - 2 * CAP)))
    send = jnp.concatenate([send_values.reshape(devices, CAP * seg_width), send_meta], axis=1)
    got = lax.all_to_all(send, ("lon", "lat"), split_axis=0, concat_axis=0, tiled=True)
    got_values = got[:, : CAP * seg_width].reshape(devices * CAP, seg_width)
    got_meta = got[:, CAP * seg_width : CAP * seg_width + 2 * CAP].reshape(devices, 2, CAP)
    got_weight = got_meta[:, 0, :].reshape(devices * CAP)
    got_offset = got_meta[:, 1, :].reshape(devices * CAP).astype(jnp.int32)

    segments = w // seg_width
    seg_local = got_offset % segments
    rest = got_offset // segments
    row_local = rest % h
    layer = rest // h
    where = jnp.stack(
        [
            layer,
            row_local // 8 * 8,
            seg_local * seg_width,
            layer % levels,
            row_local % 8,
            layer // levels,
        ],
        axis=0,
    )
    return step_call(
        where,
        got_weight,
        adjoint,
        land_mask,
        diffusivity,
        rows5,
        cols5,
        coriolis,
        got_values,
        trajectory.reshape(n_work, h, w),
    )


def solution(mesh):
    return jax.shard_map(
        per_device,
        mesh=mesh,
        in_specs=(
            P(None, None, "lat", "lon"),
            P(None, None, "lat", "lon"),
            P(None, "lat", "lon"),
            P(None, "lat", "lon"),
            P("lat"),
            P(("lon", "lat"), None),
            P(("lon", "lat")),
            P(("lon", "lat"), None),
            P(("lon", "lat")),
            P("lon"),
        ),
        out_specs=P(None, None, "lat", "lon"),
        check_vma=False,
    )
```

```python
import jax
import jax.numpy as jnp
from jax import lax
from jax.experimental import pallas as pl
from jax.experimental.pallas import tpu as pltpu
from jax.sharding import PartitionSpec as P

NSUB = 3
CAP = 8
HALO = 3
PAD_ROWS = 8
PAD_LANES = 128


def exact_dot(left, right, left_dim):
    return lax.dot_general(
        left,
        right,
        (((left_dim,), (0,)), ((), ())),
        precision=lax.Precision.HIGHEST,
        preferred_element_type=jnp.float32,
    )


def step_kernel(
    where_ref, weight_ref, adj_ref, mask_ref, diff_ref, rows_ref, cols_ref, cor_ref, vals_ref,
    traj_hbm, out_ref, xs, ds, traj_ref, sem
):
    fields = adj_ref.shape[0]
    h, w = adj_ref.shape[2], adj_ref.shape[3]
    hp, wp = xs.shape[1], xs.shape[2]
    k = pl.program_id(0)
    last = pl.num_programs(0) - 1

    @pl.when(k == 0)
    def _():
        pltpu.make_async_copy(traj_hbm, traj_ref, sem).start()

    wet = mask_ref[k].astype(jnp.float32)
    for f in range(fields):
        xs[f, 0:h, 0:w] = adj_ref[f, 0] * wet
        xs[f, h:hp, 0:w] = rows_ref[f, 0]
        xs[f, :, w:wp] = cols_ref[f, 0]
    ds[0:h, 0:w] = diff_ref[0]
    ds[h:hp, 0:w] = rows_ref[fields, 0]
    ds[:, w:wp] = cols_ref[fields, 0]
    d = ds[...]
    done = []
    for f in range(fields):
        x = xs[f]
        for _ in range(NSUB):
            east = pltpu.roll(x, wp - 1, 1)
            west = pltpu.roll(x, 1, 1)
            north = pltpu.roll(x, hp - 1, 0)
            south = pltpu.roll(x, 1, 0)
            x = x + d * (east + west + north + south - 4.0 * x)
        done.append(x[0:h, 0:w])
    rot = cor_ref[...]
    out_ref[0, k] = wet * done[0]
    out_ref[1, k] = wet * done[1]
    out_ref[2, k] = wet * (done[2] - rot * done[3])
    out_ref[3, k] = wet * (done[3] + rot * done[2])

    @pl.when(k == last)
    def _():
        pltpu.make_async_copy(traj_hbm, traj_ref, sem).wait()
        add_forcing(where_ref, weight_ref, vals_ref, traj_ref, mask_ref, out_ref)


def add_forcing(where_ref, weight_ref, vals_ref, traj_ref, mask_ref, out_ref):
    seg_width = vals_ref.shape[1]
    sub = lax.broadcasted_iota(jnp.int32, (8, seg_width), 0)

    def add_row(i, value):
        layer = where_ref[0, i]
        rows = pl.ds(pl.multiple_of(where_ref[1, i], 8), 8)
        cols = pl.ds(pl.multiple_of(where_ref[2, i], seg_width), seg_width)
        level = where_ref[3, i]
        field = where_ref[5, i]
        sampled = traj_ref[layer, rows, cols]
        misfit = weight_ref[i] * (sampled - value)
        wet = mask_ref[level, rows, cols].astype(jnp.float32)
        hit = sub == where_ref[4, i]
        cur = out_ref[field, level, rows, cols]
        out_ref[field, level, rows, cols] = cur + jnp.where(hit, wet * misfit, 0.0)

    def body(o, carry):
        first = pl.multiple_of(o * 8, 8)
        vals8 = vals_ref[pl.ds(first, 8), :]
        for j in range(8):
            add_row(first + j, vals8[j : j + 1, :])
        return carry

    lax.fori_loop(0, vals_ref.shape[0] // 8, body, 0)


def step_call(where, weight, adjoint, land_mask, diffusivity, rows5, cols5, coriolis, values, traj3):
    fields, levels, h, w = adjoint.shape
    hp, wp = h + PAD_ROWS, w + PAD_LANES
    whole = lambda shape: pl.BlockSpec(shape, lambda k, *_: (0,) * len(shape))
    return pl.pallas_call(
        step_kernel,
        grid_spec=pltpu.PrefetchScalarGridSpec(
            num_scalar_prefetch=2,
            grid=(levels,),
            in_specs=[
                pl.BlockSpec((fields, 1, h, w), lambda k, *_: (0, k, 0, 0)),
                whole(land_mask.shape),
                pl.BlockSpec((1, h, w), lambda k, *_: (k, 0, 0)),
                pl.BlockSpec((fields + 1, 1, PAD_ROWS, w), lambda k, *_: (0, k, 0, 0)),
                pl.BlockSpec((fields + 1, 1, hp, PAD_LANES), lambda k, *_: (0, k, 0, 0)),
                whole((h, 1)),
                whole(values.shape),
                pl.BlockSpec(memory_space=pl.ANY),
            ],
            out_specs=whole(adjoint.shape),
            scratch_shapes=[
                pltpu.VMEM((fields, hp, wp), jnp.float32),
                pltpu.VMEM((hp, wp), jnp.float32),
                pltpu.VMEM(traj3.shape, jnp.float32),
                pltpu.SemaphoreType.DMA(()),
            ],
        ),
        out_shape=jax.ShapeDtypeStruct(adjoint.shape, jnp.float32),
        compiler_params=pltpu.CompilerParams(vmem_limit_bytes=60 * 1024 * 1024),
    )(where, weight, adjoint, land_mask, diffusivity, rows5, cols5, coriolis.reshape(h, 1), values, traj3)


def fold_rows(top_msg, fold_partner, width):
    lon_count = lax.axis_size("lon")
    lat_count = lax.axis_size("lat")
    lon = lax.axis_index("lon")
    nx = lon_count * width
    first = lon * width
    offset = (fold_partner[0] + first - (nx - 1)) % nx
    shift_tiles = offset // width
    shift_in = offset % width
    top = lat_count - 1

    def branch(q):
        def run(msg):
            pairs_a, pairs_b = [], []
            for t in range(lon_count):
                src_a = (lon_count - 1 - t + q) % lon_count
                src_b = (src_a + 1) % lon_count
                pairs_a.append((src_a * lat_count + top, t * lat_count + top))
                pairs_b.append((src_b * lat_count + top, t * lat_count + top))
            got_a = lax.ppermute(msg, ("lon", "lat"), pairs_a)
            got_b = lax.ppermute(msg, ("lon", "lat"), pairs_b)
            return jnp.concatenate([got_a, got_b], axis=2)

        return run

    both = lax.switch(shift_tiles, [branch(q) for q in range(lon_count)], top_msg)
    source = lax.broadcasted_iota(jnp.int32, (2 * width, width), 0)
    target = lax.broadcasted_iota(jnp.int32, (2 * width, width), 1)
    pick = (source == width - 1 - target + shift_in).astype(jnp.float32)
    return exact_dot(both, pick, 2)


def per_device(
    adjoint,
    trajectory,
    diffusivity,
    land_mask,
    coriolis,
    obs_values,
    obs_weight,
    obs_owner,
    obs_offset,
    fold_partner,
):
    fields, levels, h, w = adjoint.shape
    lat_count = lax.axis_size("lat")
    lon_count = lax.axis_size("lon")
    lat = lax.axis_index("lat")
    n_work = fields * levels
    sign = jnp.array([1.0, 1.0, -1.0, -1.0], jnp.float32).reshape(fields, 1, 1, 1)

    def edge(rows):
        wet_rows = land_mask[:, rows, :].astype(jnp.float32)
        work_rows = adjoint[:, :, rows, :] * wet_rows[None]
        return work_rows, diffusivity[:, rows, :]

    top_work, top_diff = edge(slice(h - HALO, h))
    bot_work, bot_diff = edge(slice(0, HALO))
    top_msg = jnp.concatenate([top_work.reshape(n_work, HALO, w), top_diff], axis=0)
    bot_msg = jnp.concatenate([bot_work.reshape(n_work, HALO, w), bot_diff], axis=0)
    up = [(i, i + 1) for i in range(lat_count - 1)]
    down = [(i + 1, i) for i in range(lat_count - 1)]
    from_below = lax.ppermute(top_msg, "lat", up)
    from_above = lax.ppermute(bot_msg, "lat", down)
    signed_top = jnp.concatenate(
        [(top_work * sign).reshape(n_work, HALO, w), top_diff], axis=0
    )
    signed_top = jnp.concatenate(
        [signed_top[:, HALO - 1 - m : HALO - m, :] for m in range(HALO)], axis=1
    )
    folded = fold_rows(signed_top, fold_partner, w)
    north = jnp.where(lat == lat_count - 1, folded, from_above)
    gap = jnp.zeros((n_work + levels, PAD_ROWS - 2 * HALO, w), jnp.float32)
    rows_all = jnp.concatenate([north, gap, from_below], axis=1)
    rows5 = rows_all.reshape(fields + 1, levels, PAD_ROWS, w)

    lane = lax.broadcasted_iota(jnp.int32, (PAD_LANES, PAD_ROWS), 0)
    slot = lax.broadcasted_iota(jnp.int32, (PAD_LANES, PAD_ROWS), 1)
    take_first = (slot < HALO) & (lane == slot)
    take_last = (slot >= PAD_ROWS - HALO) & (lane == slot + PAD_LANES - PAD_ROWS)

    def edges(block):
        pick = lambda part, sel: jnp.einsum(
            "nyx,xc->ncy", part, sel.astype(jnp.float32), precision=lax.Precision.HIGHEST
        )
        return pick(block[..., :PAD_LANES], take_first) + pick(block[..., w - PAD_LANES :], take_last)

    wet_edges = edges(land_mask.astype(jnp.float32))
    adj_edges = edges(adjoint.reshape(n_work, h, w)).reshape(fields, levels, PAD_ROWS, h)
    work_edges = (adj_edges * wet_edges[None]).reshape(n_work, PAD_ROWS, h)
    interior = jnp.concatenate([work_edges, edges(diffusivity)], axis=0)
    col_msg = jnp.concatenate([interior, edges(rows_all)], axis=2)
    ring_west = [(i, (i - 1) % lon_count) for i in range(lon_count)]
    ring_east = [(i, (i + 1) % lon_count) for i in range(lon_count)]
    from_east = lax.ppermute(col_msg, "lon", ring_west)
    from_west = lax.ppermute(col_msg, "lon", ring_east)
    halo_slot = lax.broadcasted_iota(jnp.int32, col_msg.shape, 1)
    got_cols = jnp.where(halo_slot < HALO, from_east, from_west)
    place = (take_first | take_last).astype(jnp.float32).T
    cols5 = jnp.einsum("ncy,cl->nyl", got_cols, place, precision=lax.Precision.HIGHEST)
    cols5 = cols5.reshape(fields + 1, levels, h + PAD_ROWS, PAD_LANES)


    devices = lon_count * lat_count
    _, _, obs_values, obs_weight, obs_owner, obs_offset = lax.optimization_barrier(
        (top_msg, bot_msg, obs_values, obs_weight, obs_owner, obs_offset)
    )
    seg_width = obs_values.shape[1]
    rows_sent = obs_values.shape[0]
    owner_index = obs_owner[:, 0]
    one_hot = (owner_index[:, None] == jnp.arange(devices, dtype=jnp.int32)[None, :]).astype(
        jnp.bfloat16
    )
    row_ids = jnp.arange(rows_sent, dtype=jnp.int32)
    before = (row_ids[None, :] < row_ids[:, None]).astype(jnp.bfloat16)
    earlier = lax.dot_general(
        before, one_hot, (((1,), (0,)), ((), ())), preferred_element_type=jnp.float32
    )
    slot_index = jnp.sum(earlier * one_hot.astype(jnp.float32), axis=1).astype(jnp.int32)
    dest_index = owner_index * CAP + slot_index
    slot_ids = jnp.arange(devices * CAP, dtype=jnp.int32)
    placement = (dest_index[:, None] == slot_ids[None, :]).astype(jnp.float32)
    send_values = exact_dot(placement, obs_values, 0).reshape(devices, CAP, seg_width)
    meta = jnp.stack([obs_weight, obs_offset.astype(jnp.float32)], axis=1)
    send_meta = exact_dot(placement, meta, 0).reshape(devices, CAP, 2)
    send_meta = jnp.swapaxes(send_meta, 1, 2).reshape(devices, 2 * CAP)
    send_meta = jnp.pad(send_meta, ((0, 0), (0, seg_width - 2 * CAP)))
    send = jnp.concatenate([send_values.reshape(devices, CAP * seg_width), send_meta], axis=1)
    got = lax.all_to_all(send, ("lon", "lat"), split_axis=0, concat_axis=0, tiled=True)
    got_values = got[:, : CAP * seg_width].reshape(devices * CAP, seg_width)
    got_meta = got[:, CAP * seg_width : CAP * seg_width + 2 * CAP].reshape(devices, 2, CAP)
    got_weight = got_meta[:, 0, :].reshape(devices * CAP)
    got_offset = got_meta[:, 1, :].reshape(devices * CAP).astype(jnp.int32)

    segments = w // seg_width
    seg_local = got_offset % segments
    rest = got_offset // segments
    row_local = rest % h
    layer = rest // h
    where = jnp.stack(
        [
            layer,
            row_local // 8 * 8,
            seg_local * seg_width,
            layer % levels,
            row_local % 8,
            layer // levels,
        ],
        axis=0,
    )
    return step_call(
        where,
        got_weight,
        adjoint,
        land_mask,
        diffusivity,
        rows5,
        cols5,
        coriolis,
        got_values,
        trajectory.reshape(n_work, h, w),
    )


def solution(mesh):
    return jax.shard_map(
        per_device,
        mesh=mesh,
        in_specs=(
            P(None, None, "lat", "lon"),
            P(None, None, "lat", "lon"),
            P(None, "lat", "lon"),
            P(None, "lat", "lon"),
            P("lat"),
            P(("lon", "lat"), None),
            P(("lon", "lat")),
            P(("lon", "lat"), None),
            P(("lon", "lat")),
            P("lon"),
        ),
        out_specs=P(None, None, "lat", "lon"),
        check_vma=False,
    )
```

```python
import jax
import jax.numpy as jnp
from jax import lax
from jax.experimental import pallas as pl
from jax.experimental.pallas import tpu as pltpu
from jax.sharding import PartitionSpec as P

NSUB = 3
CAP = 8
HALO = 3
PAD_ROWS = 8
PAD_LANES = 128


def exact_dot(left, right, left_dim):
    return lax.dot_general(
        left,
        right,
        (((left_dim,), (0,)), ((), ())),
        precision=lax.Precision.HIGHEST,
        preferred_element_type=jnp.float32,
    )


def step_kernel(
    tiles_ref,
    where_ref, weight_ref, adj_ref, mask_ref, diff_ref, rows_ref, cols_ref, cor_ref, vals_ref,
    traj_hbm, out_ref, xs, ds, traj_ref, sem
):
    fields = adj_ref.shape[0]
    h, w = adj_ref.shape[2], adj_ref.shape[3]
    hp, wp = xs.shape[1], xs.shape[2]
    k = pl.program_id(0)
    last = pl.num_programs(0) - 1

    @pl.when(k == 0)
    def _():
        pltpu.make_async_copy(traj_hbm, traj_ref, sem).start()

    wet = mask_ref[k].astype(jnp.float32)
    for f in range(fields):
        xs[f, 0:h, 0:w] = adj_ref[f, 0] * wet
        xs[f, h:hp, 0:w] = rows_ref[f, 0]
        xs[f, :, w:wp] = cols_ref[f, 0]
    ds[0:h, 0:w] = diff_ref[0]
    ds[h:hp, 0:w] = rows_ref[fields, 0]
    ds[:, w:wp] = cols_ref[fields, 0]
    d = ds[...]
    done = []
    for f in range(fields):
        x = xs[f]
        for _ in range(NSUB):
            east = pltpu.roll(x, wp - 1, 1)
            west = pltpu.roll(x, 1, 1)
            north = pltpu.roll(x, hp - 1, 0)
            south = pltpu.roll(x, 1, 0)
            x = x + d * (east + west + north + south - 4.0 * x)
        done.append(x[0:h, 0:w])
    rot = cor_ref[...]
    out_ref[0, k] = wet * done[0]
    out_ref[1, k] = wet * done[1]
    out_ref[2, k] = wet * (done[2] - rot * done[3])
    out_ref[3, k] = wet * (done[3] + rot * done[2])

    @pl.when(k == last)
    def _():
        pltpu.make_async_copy(traj_hbm, traj_ref, sem).wait()
        add_forcing(tiles_ref[0], where_ref, weight_ref, vals_ref, traj_ref, mask_ref, out_ref)


def add_forcing(tiles, where_ref, weight_ref, vals_ref, traj_ref, mask_ref, out_ref):
    seg_width = vals_ref.shape[1]
    sub = lax.broadcasted_iota(jnp.int32, (8, seg_width), 0)

    def add_row(i, value):
        layer = where_ref[0, i]
        rows = pl.ds(pl.multiple_of(where_ref[1, i], 8), 8)
        cols = pl.ds(pl.multiple_of(where_ref[2, i], seg_width), seg_width)
        level = where_ref[3, i]
        field = where_ref[5, i]
        sampled = traj_ref[layer, rows, cols]
        misfit = weight_ref[i] * (sampled - value)
        wet = mask_ref[level, rows, cols].astype(jnp.float32)
        hit = sub == where_ref[4, i]
        cur = out_ref[field, level, rows, cols]
        out_ref[field, level, rows, cols] = cur + jnp.where(hit, wet * misfit, 0.0)

    def body(o, carry):
        first = pl.multiple_of(o * 8, 8)
        vals8 = vals_ref[pl.ds(first, 8), :]
        for j in range(8):
            add_row(first + j, vals8[j : j + 1, :])
        return carry

    lax.fori_loop(0, tiles, body, 0)


def step_call(tiles, where, weight, adjoint, land_mask, diffusivity, rows5, cols5, coriolis, values, traj3):
    fields, levels, h, w = adjoint.shape
    hp, wp = h + PAD_ROWS, w + PAD_LANES
    whole = lambda shape: pl.BlockSpec(shape, lambda k, *_: (0,) * len(shape))
    return pl.pallas_call(
        step_kernel,
        grid_spec=pltpu.PrefetchScalarGridSpec(
            num_scalar_prefetch=3,
            grid=(levels,),
            in_specs=[
                pl.BlockSpec((fields, 1, h, w), lambda k, *_: (0, k, 0, 0)),
                whole(land_mask.shape),
                pl.BlockSpec((1, h, w), lambda k, *_: (k, 0, 0)),
                pl.BlockSpec((fields + 1, 1, PAD_ROWS, w), lambda k, *_: (0, k, 0, 0)),
                pl.BlockSpec((fields + 1, 1, hp, PAD_LANES), lambda k, *_: (0, k, 0, 0)),
                whole((h, 1)),
                whole(values.shape),
                pl.BlockSpec(memory_space=pl.ANY),
            ],
            out_specs=whole(adjoint.shape),
            scratch_shapes=[
                pltpu.VMEM((fields, hp, wp), jnp.float32),
                pltpu.VMEM((hp, wp), jnp.float32),
                pltpu.VMEM(traj3.shape, jnp.float32),
                pltpu.SemaphoreType.DMA(()),
            ],
        ),
        out_shape=jax.ShapeDtypeStruct(adjoint.shape, jnp.float32),
        compiler_params=pltpu.CompilerParams(vmem_limit_bytes=60 * 1024 * 1024),
    )(tiles, where, weight, adjoint, land_mask, diffusivity, rows5, cols5, coriolis.reshape(h, 1), values, traj3)


def fold_rows(top_msg, fold_partner, width):
    lon_count = lax.axis_size("lon")
    lat_count = lax.axis_size("lat")
    lon = lax.axis_index("lon")
    nx = lon_count * width
    first = lon * width
    offset = (fold_partner[0] + first - (nx - 1)) % nx
    shift_tiles = offset // width
    shift_in = offset % width
    top = lat_count - 1

    def branch(q):
        def run(msg):
            pairs_a, pairs_b = [], []
            for t in range(lon_count):
                src_a = (lon_count - 1 - t + q) % lon_count
                src_b = (src_a + 1) % lon_count
                pairs_a.append((src_a * lat_count + top, t * lat_count + top))
                pairs_b.append((src_b * lat_count + top, t * lat_count + top))
            got_a = lax.ppermute(msg, ("lon", "lat"), pairs_a)
            got_b = lax.ppermute(msg, ("lon", "lat"), pairs_b)
            return jnp.concatenate([got_a, got_b], axis=2)

        return run

    both = lax.switch(shift_tiles, [branch(q) for q in range(lon_count)], top_msg)
    source = lax.broadcasted_iota(jnp.int32, (2 * width, width), 0)
    target = lax.broadcasted_iota(jnp.int32, (2 * width, width), 1)
    pick = (source == width - 1 - target + shift_in).astype(jnp.float32)
    return exact_dot(both, pick, 2)


def per_device(
    adjoint,
    trajectory,
    diffusivity,
    land_mask,
    coriolis,
    obs_values,
    obs_weight,
    obs_owner,
    obs_offset,
    fold_partner,
):
    fields, levels, h, w = adjoint.shape
    lat_count = lax.axis_size("lat")
    lon_count = lax.axis_size("lon")
    lat = lax.axis_index("lat")
    n_work = fields * levels
    sign = jnp.array([1.0, 1.0, -1.0, -1.0], jnp.float32).reshape(fields, 1, 1, 1)

    def edge(rows):
        wet_rows = land_mask[:, rows, :].astype(jnp.float32)
        work_rows = adjoint[:, :, rows, :] * wet_rows[None]
        return work_rows, diffusivity[:, rows, :]

    top_work, top_diff = edge(slice(h - HALO, h))
    bot_work, bot_diff = edge(slice(0, HALO))
    top_msg = jnp.concatenate([top_work.reshape(n_work, HALO, w), top_diff], axis=0)
    bot_msg = jnp.concatenate([bot_work.reshape(n_work, HALO, w), bot_diff], axis=0)
    up = [(i, i + 1) for i in range(lat_count - 1)]
    down = [(i + 1, i) for i in range(lat_count - 1)]
    from_below = lax.ppermute(top_msg, "lat", up)
    from_above = lax.ppermute(bot_msg, "lat", down)
    signed_top = jnp.concatenate(
        [(top_work * sign).reshape(n_work, HALO, w), top_diff], axis=0
    )
    signed_top = jnp.concatenate(
        [signed_top[:, HALO - 1 - m : HALO - m, :] for m in range(HALO)], axis=1
    )
    folded = fold_rows(signed_top, fold_partner, w)
    north = jnp.where(lat == lat_count - 1, folded, from_above)
    gap = jnp.zeros((n_work + levels, PAD_ROWS - 2 * HALO, w), jnp.float32)
    rows_all = jnp.concatenate([north, gap, from_below], axis=1)
    rows5 = rows_all.reshape(fields + 1, levels, PAD_ROWS, w)

    lane = lax.broadcasted_iota(jnp.int32, (PAD_LANES, PAD_ROWS), 0)
    slot = lax.broadcasted_iota(jnp.int32, (PAD_LANES, PAD_ROWS), 1)
    take_first = (slot < HALO) & (lane == slot)
    take_last = (slot >= PAD_ROWS - HALO) & (lane == slot + PAD_LANES - PAD_ROWS)

    def edges(block):
        pick = lambda part, sel: jnp.einsum(
            "nyx,xc->ncy", part, sel.astype(jnp.float32), precision=lax.Precision.HIGHEST
        )
        return pick(block[..., :PAD_LANES], take_first) + pick(block[..., w - PAD_LANES :], take_last)

    wet_edges = edges(land_mask.astype(jnp.float32))
    adj_edges = edges(adjoint.reshape(n_work, h, w)).reshape(fields, levels, PAD_ROWS, h)
    work_edges = (adj_edges * wet_edges[None]).reshape(n_work, PAD_ROWS, h)
    interior = jnp.concatenate([work_edges, edges(diffusivity)], axis=0)
    col_msg = jnp.concatenate([interior, edges(rows_all)], axis=2)
    ring_west = [(i, (i - 1) % lon_count) for i in range(lon_count)]
    ring_east = [(i, (i + 1) % lon_count) for i in range(lon_count)]
    from_east = lax.ppermute(col_msg, "lon", ring_west)
    from_west = lax.ppermute(col_msg, "lon", ring_east)
    halo_slot = lax.broadcasted_iota(jnp.int32, col_msg.shape, 1)
    got_cols = jnp.where(halo_slot < HALO, from_east, from_west)
    place = (take_first | take_last).astype(jnp.float32).T
    cols5 = jnp.einsum("ncy,cl->nyl", got_cols, place, precision=lax.Precision.HIGHEST)
    cols5 = cols5.reshape(fields + 1, levels, h + PAD_ROWS, PAD_LANES)


    devices = lon_count * lat_count
    seg_width = obs_values.shape[1]
    rows_sent = obs_values.shape[0]
    owner_index = obs_owner[:, 0]
    one_hot = (owner_index[:, None] == jnp.arange(devices, dtype=jnp.int32)[None, :]).astype(
        jnp.bfloat16
    )
    row_ids = jnp.arange(rows_sent, dtype=jnp.int32)
    before = (row_ids[None, :] < row_ids[:, None]).astype(jnp.bfloat16)
    earlier = lax.dot_general(
        before, one_hot, (((1,), (0,)), ((), ())), preferred_element_type=jnp.float32
    )
    slot_index = jnp.sum(earlier * one_hot.astype(jnp.float32), axis=1).astype(jnp.int32)
    dest_index = owner_index * CAP + slot_index
    slot_ids = jnp.arange(devices * CAP, dtype=jnp.int32)
    placement = (dest_index[:, None] == slot_ids[None, :]).astype(jnp.float32)
    send_values = exact_dot(placement, obs_values, 0).reshape(devices, CAP, seg_width)
    meta = jnp.stack([obs_weight, obs_offset.astype(jnp.float32)], axis=1)
    send_meta = exact_dot(placement, meta, 0).reshape(devices, CAP, 2)
    send_meta = jnp.swapaxes(send_meta, 1, 2).reshape(devices, 2 * CAP)
    send_meta = jnp.pad(send_meta, ((0, 0), (0, seg_width - 2 * CAP)))
    send = jnp.concatenate([send_values.reshape(devices, CAP * seg_width), send_meta], axis=1)
    got = lax.all_to_all(send, ("lon", "lat"), split_axis=0, concat_axis=0, tiled=True)
    got_values = got[:, : CAP * seg_width].reshape(devices * CAP, seg_width)
    got_meta = got[:, CAP * seg_width : CAP * seg_width + 2 * CAP].reshape(devices, 2, CAP)
    got_weight = got_meta[:, 0, :].reshape(devices * CAP)
    got_offset = got_meta[:, 1, :].reshape(devices * CAP)
    n_slots = devices * CAP
    filled = got_weight != 0.0
    slot_order = jnp.arange(n_slots, dtype=jnp.int32)
    earlier_slots = (slot_order[None, :] < slot_order[:, None]).astype(jnp.bfloat16)
    packed_at = lax.dot_general(
        earlier_slots,
        filled.astype(jnp.bfloat16)[:, None],
        (((1,), (0,)), ((), ())),
        preferred_element_type=jnp.float32,
    )[:, 0].astype(jnp.int32)
    pack = ((packed_at[None, :] == slot_order[:, None]) & filled[None, :]).astype(jnp.float32)
    payload = jnp.concatenate([got_values, got_weight[:, None], got_offset[:, None]], axis=1)
    packed = exact_dot(pack, payload, 1)
    got_values = packed[:, :seg_width]
    got_weight = packed[:, seg_width]
    got_offset = packed[:, seg_width + 1].astype(jnp.int32)
    n_filled = jnp.sum(filled.astype(jnp.int32))
    tiles = ((n_filled + 7) // 8).reshape(1)

    segments = w // seg_width
    seg_local = got_offset % segments
    rest = got_offset // segments
    row_local = rest % h
    layer = rest // h
    where = jnp.stack(
        [
            layer,
            row_local // 8 * 8,
            seg_local * seg_width,
            layer % levels,
            row_local % 8,
            layer // levels,
        ],
        axis=0,
    )
    return step_call(
        tiles,
        where,
        got_weight,
        adjoint,
        land_mask,
        diffusivity,
        rows5,
        cols5,
        coriolis,
        got_values,
        trajectory.reshape(n_work, h, w),
    )


def solution(mesh):
    return jax.shard_map(
        per_device,
        mesh=mesh,
        in_specs=(
            P(None, None, "lat", "lon"),
            P(None, None, "lat", "lon"),
            P(None, "lat", "lon"),
            P(None, "lat", "lon"),
            P("lat"),
            P(("lon", "lat"), None),
            P(("lon", "lat")),
            P(("lon", "lat"), None),
            P(("lon", "lat")),
            P("lon"),
        ),
        out_specs=P(None, None, "lat", "lon"),
        check_vma=False,
    )
```

```python
import jax
import jax.numpy as jnp
from jax import lax
from jax.experimental import pallas as pl
from jax.experimental.pallas import tpu as pltpu
from jax.sharding import PartitionSpec as P

NSUB = 3
CAP = 8
HALO = 3
PAD_ROWS = 8
PAD_LANES = 128


def exact_dot(left, right, left_dim):
    return lax.dot_general(
        left,
        right,
        (((left_dim,), (0,)), ((), ())),
        precision=lax.Precision.HIGHEST,
        preferred_element_type=jnp.float32,
    )


def step_kernel(
    where_ref, weight_ref, adj_ref, mask_ref, diff_ref, rows_ref, cols_ref, cor_ref, vals_ref,
    traj_ref, out_ref, xs, ds
):
    fields = adj_ref.shape[0]
    h, w = adj_ref.shape[2], adj_ref.shape[3]
    hp, wp = xs.shape[1], xs.shape[2]
    k = pl.program_id(0)
    per_step = vals_ref.shape[0] // pl.num_programs(0)

    @pl.when(k == 0)
    def _():
        out_ref[...] = jnp.zeros(out_ref.shape, jnp.float32)

    add_forcing(k * per_step, per_step, where_ref, weight_ref, vals_ref, traj_ref, mask_ref, out_ref)

    wet = mask_ref[k].astype(jnp.float32)
    for f in range(fields):
        xs[f, 0:h, 0:w] = adj_ref[f, 0] * wet
        xs[f, h:hp, 0:w] = rows_ref[f, 0]
        xs[f, :, w:wp] = cols_ref[f, 0]
    ds[0:h, 0:w] = diff_ref[0]
    ds[h:hp, 0:w] = rows_ref[fields, 0]
    ds[:, w:wp] = cols_ref[fields, 0]
    d = ds[...]
    done = []
    for f in range(fields):
        x = xs[f]
        for _ in range(NSUB):
            east = pltpu.roll(x, wp - 1, 1)
            west = pltpu.roll(x, 1, 1)
            north = pltpu.roll(x, hp - 1, 0)
            south = pltpu.roll(x, 1, 0)
            x = x + d * (east + west + north + south - 4.0 * x)
        done.append(x[0:h, 0:w])
    rot = cor_ref[...]
    out_ref[0, k] = out_ref[0, k] + wet * done[0]
    out_ref[1, k] = out_ref[1, k] + wet * done[1]
    out_ref[2, k] = out_ref[2, k] + wet * (done[2] - rot * done[3])
    out_ref[3, k] = out_ref[3, k] + wet * (done[3] + rot * done[2])


def add_forcing(start, count, where_ref, weight_ref, vals_ref, traj_ref, mask_ref, out_ref):
    seg_width = vals_ref.shape[1]
    sub = lax.broadcasted_iota(jnp.int32, (8, seg_width), 0)

    def add_row(i, value):
        layer = where_ref[0, i]
        rows = pl.ds(pl.multiple_of(where_ref[1, i], 8), 8)
        cols = pl.ds(pl.multiple_of(where_ref[2, i], seg_width), seg_width)
        level = where_ref[3, i]
        field = where_ref[5, i]
        sampled = traj_ref[layer, rows, cols]
        misfit = weight_ref[i] * (sampled - value)
        wet = mask_ref[level, rows, cols].astype(jnp.float32)
        hit = sub == where_ref[4, i]
        cur = out_ref[field, level, rows, cols]
        out_ref[field, level, rows, cols] = cur + jnp.where(hit, wet * misfit, 0.0)

    for t in range(count // 8):
        first = pl.multiple_of(start + 8 * t, 8)
        vals8 = vals_ref[pl.ds(first, 8), :]
        for j in range(8):
            add_row(first + j, vals8[j : j + 1, :])


def step_call(where, weight, adjoint, land_mask, diffusivity, rows5, cols5, coriolis, values, traj3):
    fields, levels, h, w = adjoint.shape
    hp, wp = h + PAD_ROWS, w + PAD_LANES
    rows_in = values.shape[0]
    per_step = -(-(-(-rows_in // levels)) // 8) * 8
    extra = per_step * levels - rows_in
    values = jnp.pad(values, ((0, extra), (0, 0)))
    weight = jnp.pad(weight, (0, extra))
    where = jnp.pad(where, ((0, 0), (0, extra)))
    whole = lambda shape: pl.BlockSpec(shape, lambda k, *_: (0,) * len(shape))
    return pl.pallas_call(
        step_kernel,
        grid_spec=pltpu.PrefetchScalarGridSpec(
            num_scalar_prefetch=2,
            grid=(levels,),
            in_specs=[
                pl.BlockSpec((fields, 1, h, w), lambda k, *_: (0, k, 0, 0)),
                whole(land_mask.shape),
                pl.BlockSpec((1, h, w), lambda k, *_: (k, 0, 0)),
                pl.BlockSpec((fields + 1, 1, PAD_ROWS, w), lambda k, *_: (0, k, 0, 0)),
                pl.BlockSpec((fields + 1, 1, hp, PAD_LANES), lambda k, *_: (0, k, 0, 0)),
                whole((h, 1)),
                whole(values.shape),
                whole(traj3.shape),
            ],
            out_specs=whole(adjoint.shape),
            scratch_shapes=[
                pltpu.VMEM((fields, hp, wp), jnp.float32),
                pltpu.VMEM((hp, wp), jnp.float32),
            ],
        ),
        out_shape=jax.ShapeDtypeStruct(adjoint.shape, jnp.float32),
        compiler_params=pltpu.CompilerParams(vmem_limit_bytes=60 * 1024 * 1024),
    )(where, weight, adjoint, land_mask, diffusivity, rows5, cols5, coriolis.reshape(h, 1), values, traj3)


def fold_rows(top_msg, fold_partner, width):
    lon_count = lax.axis_size("lon")
    lat_count = lax.axis_size("lat")
    lon = lax.axis_index("lon")
    nx = lon_count * width
    first = lon * width
    offset = (fold_partner[0] + first - (nx - 1)) % nx
    shift_tiles = offset // width
    shift_in = offset % width
    top = lat_count - 1

    def branch(q):
        def run(msg):
            pairs_a, pairs_b = [], []
            for t in range(lon_count):
                src_a = (lon_count - 1 - t + q) % lon_count
                src_b = (src_a + 1) % lon_count
                pairs_a.append((src_a * lat_count + top, t * lat_count + top))
                pairs_b.append((src_b * lat_count + top, t * lat_count + top))
            got_a = lax.ppermute(msg, ("lon", "lat"), pairs_a)
            got_b = lax.ppermute(msg, ("lon", "lat"), pairs_b)
            return jnp.concatenate([got_a, got_b], axis=2)

        return run

    both = lax.switch(shift_tiles, [branch(q) for q in range(lon_count)], top_msg)
    source = lax.broadcasted_iota(jnp.int32, (2 * width, width), 0)
    target = lax.broadcasted_iota(jnp.int32, (2 * width, width), 1)
    pick = (source == width - 1 - target + shift_in).astype(jnp.float32)
    return exact_dot(both, pick, 2)


def per_device(
    adjoint,
    trajectory,
    diffusivity,
    land_mask,
    coriolis,
    obs_values,
    obs_weight,
    obs_owner,
    obs_offset,
    fold_partner,
):
    fields, levels, h, w = adjoint.shape
    lat_count = lax.axis_size("lat")
    lon_count = lax.axis_size("lon")
    lat = lax.axis_index("lat")
    n_work = fields * levels
    sign = jnp.array([1.0, 1.0, -1.0, -1.0], jnp.float32).reshape(fields, 1, 1, 1)

    def edge(rows):
        wet_rows = land_mask[:, rows, :].astype(jnp.float32)
        work_rows = adjoint[:, :, rows, :] * wet_rows[None]
        return work_rows, diffusivity[:, rows, :]

    top_work, top_diff = edge(slice(h - HALO, h))
    bot_work, bot_diff = edge(slice(0, HALO))
    top_msg = jnp.concatenate([top_work.reshape(n_work, HALO, w), top_diff], axis=0)
    bot_msg = jnp.concatenate([bot_work.reshape(n_work, HALO, w), bot_diff], axis=0)
    up = [(i, i + 1) for i in range(lat_count - 1)]
    down = [(i + 1, i) for i in range(lat_count - 1)]
    from_below = lax.ppermute(top_msg, "lat", up)
    from_above = lax.ppermute(bot_msg, "lat", down)
    signed_top = jnp.concatenate(
        [(top_work * sign).reshape(n_work, HALO, w), top_diff], axis=0
    )
    signed_top = jnp.concatenate(
        [signed_top[:, HALO - 1 - m : HALO - m, :] for m in range(HALO)], axis=1
    )
    folded = fold_rows(signed_top, fold_partner, w)
    north = jnp.where(lat == lat_count - 1, folded, from_above)
    gap = jnp.zeros((n_work + levels, PAD_ROWS - 2 * HALO, w), jnp.float32)
    rows_all = jnp.concatenate([north, gap, from_below], axis=1)
    rows5 = rows_all.reshape(fields + 1, levels, PAD_ROWS, w)

    lane = lax.broadcasted_iota(jnp.int32, (PAD_LANES, PAD_ROWS), 0)
    slot = lax.broadcasted_iota(jnp.int32, (PAD_LANES, PAD_ROWS), 1)
    take_first = (slot < HALO) & (lane == slot)
    take_last = (slot >= PAD_ROWS - HALO) & (lane == slot + PAD_LANES - PAD_ROWS)

    def edges(block):
        pick = lambda part, sel: jnp.einsum(
            "nyx,xc->ncy", part, sel.astype(jnp.float32), precision=lax.Precision.HIGHEST
        )
        return pick(block[..., :PAD_LANES], take_first) + pick(block[..., w - PAD_LANES :], take_last)

    wet_edges = edges(land_mask.astype(jnp.float32))
    adj_edges = edges(adjoint.reshape(n_work, h, w)).reshape(fields, levels, PAD_ROWS, h)
    work_edges = (adj_edges * wet_edges[None]).reshape(n_work, PAD_ROWS, h)
    interior = jnp.concatenate([work_edges, edges(diffusivity)], axis=0)
    col_msg = jnp.concatenate([interior, edges(rows_all)], axis=2)
    ring_west = [(i, (i - 1) % lon_count) for i in range(lon_count)]
    ring_east = [(i, (i + 1) % lon_count) for i in range(lon_count)]
    from_east = lax.ppermute(col_msg, "lon", ring_west)
    from_west = lax.ppermute(col_msg, "lon", ring_east)
    halo_slot = lax.broadcasted_iota(jnp.int32, col_msg.shape, 1)
    got_cols = jnp.where(halo_slot < HALO, from_east, from_west)
    place = (take_first | take_last).astype(jnp.float32).T
    cols5 = jnp.einsum("ncy,cl->nyl", got_cols, place, precision=lax.Precision.HIGHEST)
    cols5 = cols5.reshape(fields + 1, levels, h + PAD_ROWS, PAD_LANES)


    devices = lon_count * lat_count
    seg_width = obs_values.shape[1]
    rows_sent = obs_values.shape[0]
    owner_index = obs_owner[:, 0]
    one_hot = (owner_index[:, None] == jnp.arange(devices, dtype=jnp.int32)[None, :]).astype(
        jnp.bfloat16
    )
    row_ids = jnp.arange(rows_sent, dtype=jnp.int32)
    before = (row_ids[None, :] < row_ids[:, None]).astype(jnp.bfloat16)
    earlier = lax.dot_general(
        before, one_hot, (((1,), (0,)), ((), ())), preferred_element_type=jnp.float32
    )
    slot_index = jnp.sum(earlier * one_hot.astype(jnp.float32), axis=1).astype(jnp.int32)
    dest_index = owner_index * CAP + slot_index
    slot_ids = jnp.arange(devices * CAP, dtype=jnp.int32)
    placement = (dest_index[:, None] == slot_ids[None, :]).astype(jnp.float32)
    send_values = exact_dot(placement, obs_values, 0).reshape(devices, CAP, seg_width)
    meta = jnp.stack([obs_weight, obs_offset.astype(jnp.float32)], axis=1)
    send_meta = exact_dot(placement, meta, 0).reshape(devices, CAP, 2)
    send_meta = jnp.swapaxes(send_meta, 1, 2).reshape(devices, 2 * CAP)
    send_meta = jnp.pad(send_meta, ((0, 0), (0, seg_width - 2 * CAP)))
    send = jnp.concatenate([send_values.reshape(devices, CAP * seg_width), send_meta], axis=1)
    got = lax.all_to_all(send, ("lon", "lat"), split_axis=0, concat_axis=0, tiled=True)
    got_values = got[:, : CAP * seg_width].reshape(devices * CAP, seg_width)
    got_meta = got[:, CAP * seg_width : CAP * seg_width + 2 * CAP].reshape(devices, 2, CAP)
    got_weight = got_meta[:, 0, :].reshape(devices * CAP)
    got_offset = got_meta[:, 1, :].reshape(devices * CAP).astype(jnp.int32)

    segments = w // seg_width
    seg_local = got_offset % segments
    rest = got_offset // segments
    row_local = rest % h
    layer = rest // h
    where = jnp.stack(
        [
            layer,
            row_local // 8 * 8,
            seg_local * seg_width,
            layer % levels,
            row_local % 8,
            layer // levels,
        ],
        axis=0,
    )
    return step_call(
        where,
        got_weight,
        adjoint,
        land_mask,
        diffusivity,
        rows5,
        cols5,
        coriolis,
        got_values,
        trajectory.reshape(n_work, h, w),
    )


def solution(mesh):
    return jax.shard_map(
        per_device,
        mesh=mesh,
        in_specs=(
            P(None, None, "lat", "lon"),
            P(None, None, "lat", "lon"),
            P(None, "lat", "lon"),
            P(None, "lat", "lon"),
            P("lat"),
            P(("lon", "lat"), None),
            P(("lon", "lat")),
            P(("lon", "lat"), None),
            P(("lon", "lat")),
            P("lon"),
        ),
        out_specs=P(None, None, "lat", "lon"),
        check_vma=False,
    )
```

```python
import jax
import jax.numpy as jnp
from jax import lax
from jax.experimental import pallas as pl
from jax.experimental.pallas import tpu as pltpu
from jax.sharding import PartitionSpec as P

NSUB = 3
CAP = 8
HALO = 3
PAD_ROWS = 8
PAD_LANES = 128


def exact_dot(left, right, left_dim):
    return lax.dot_general(
        left,
        right,
        (((left_dim,), (0,)), ((), ())),
        precision=lax.Precision.HIGHEST,
        preferred_element_type=jnp.float32,
    )


def exact_pick(spec, data, onehot):
    hi = data.astype(jnp.bfloat16)
    rest = data - hi.astype(jnp.float32)
    mid = rest.astype(jnp.bfloat16)
    lo = (rest - mid.astype(jnp.float32)).astype(jnp.bfloat16)
    sel = onehot.astype(jnp.bfloat16)
    part = lambda piece: jnp.einsum(spec, piece, sel, preferred_element_type=jnp.float32)
    return (part(hi) + part(mid)) + part(lo)


def step_kernel(
    where_ref, weight_ref, adj_ref, mask_ref, diff_ref, rows_ref, cols_ref, cor_ref, vals_ref,
    traj_ref, out_ref, xs, ds
):
    fields = adj_ref.shape[0]
    h, w = adj_ref.shape[2], adj_ref.shape[3]
    hp, wp = xs.shape[1], xs.shape[2]
    k = pl.program_id(0)
    per_step = vals_ref.shape[0] // pl.num_programs(0)

    @pl.when(k == 0)
    def _():
        out_ref[...] = jnp.zeros(out_ref.shape, jnp.float32)

    add_forcing(k * per_step, per_step, where_ref, weight_ref, vals_ref, traj_ref, mask_ref, out_ref)

    wet = mask_ref[k].astype(jnp.float32)
    for f in range(fields):
        xs[f, 0:h, 0:w] = adj_ref[f, 0] * wet
        xs[f, h:hp, 0:w] = rows_ref[f, 0]
        xs[f, :, w:wp] = cols_ref[f, 0]
    ds[0:h, 0:w] = diff_ref[0]
    ds[h:hp, 0:w] = rows_ref[fields, 0]
    ds[:, w:wp] = cols_ref[fields, 0]
    d = ds[...]
    done = []
    for f in range(fields):
        x = xs[f]
        for _ in range(NSUB):
            east = pltpu.roll(x, wp - 1, 1)
            west = pltpu.roll(x, 1, 1)
            north = pltpu.roll(x, hp - 1, 0)
            south = pltpu.roll(x, 1, 0)
            x = x + d * (east + west + north + south - 4.0 * x)
        done.append(x[0:h, 0:w])
    rot = cor_ref[...]
    out_ref[0, k] = out_ref[0, k] + wet * done[0]
    out_ref[1, k] = out_ref[1, k] + wet * done[1]
    out_ref[2, k] = out_ref[2, k] + wet * (done[2] - rot * done[3])
    out_ref[3, k] = out_ref[3, k] + wet * (done[3] + rot * done[2])


def add_forcing(start, count, where_ref, weight_ref, vals_ref, traj_ref, mask_ref, out_ref):
    seg_width = vals_ref.shape[1]
    sub = lax.broadcasted_iota(jnp.int32, (8, seg_width), 0)

    def add_row(i, value):
        layer = where_ref[0, i]
        rows = pl.ds(pl.multiple_of(where_ref[1, i], 8), 8)
        cols = pl.ds(pl.multiple_of(where_ref[2, i], seg_width), seg_width)
        level = where_ref[3, i]
        field = where_ref[5, i]
        sampled = traj_ref[layer, rows, cols]
        misfit = weight_ref[i] * (sampled - value)
        wet = mask_ref[level, rows, cols].astype(jnp.float32)
        hit = sub == where_ref[4, i]
        cur = out_ref[field, level, rows, cols]
        out_ref[field, level, rows, cols] = cur + jnp.where(hit, wet * misfit, 0.0)

    for t in range(count // 8):
        first = pl.multiple_of(start + 8 * t, 8)
        vals8 = vals_ref[pl.ds(first, 8), :]
        for j in range(8):
            add_row(first + j, vals8[j : j + 1, :])


def step_call(where, weight, adjoint, land_mask, diffusivity, rows5, cols5, coriolis, values, traj3):
    fields, levels, h, w = adjoint.shape
    hp, wp = h + PAD_ROWS, w + PAD_LANES
    rows_in = values.shape[0]
    per_step = -(-(-(-rows_in // levels)) // 8) * 8
    extra = per_step * levels - rows_in
    values = jnp.pad(values, ((0, extra), (0, 0)))
    weight = jnp.pad(weight, (0, extra))
    where = jnp.pad(where, ((0, 0), (0, extra)))
    whole = lambda shape: pl.BlockSpec(shape, lambda k, *_: (0,) * len(shape))
    return pl.pallas_call(
        step_kernel,
        grid_spec=pltpu.PrefetchScalarGridSpec(
            num_scalar_prefetch=2,
            grid=(levels,),
            in_specs=[
                pl.BlockSpec((fields, 1, h, w), lambda k, *_: (0, k, 0, 0)),
                whole(land_mask.shape),
                pl.BlockSpec((1, h, w), lambda k, *_: (k, 0, 0)),
                pl.BlockSpec((fields + 1, 1, PAD_ROWS, w), lambda k, *_: (0, k, 0, 0)),
                pl.BlockSpec((fields + 1, 1, hp, PAD_LANES), lambda k, *_: (0, k, 0, 0)),
                whole((h, 1)),
                whole(values.shape),
                whole(traj3.shape),
            ],
            out_specs=whole(adjoint.shape),
            scratch_shapes=[
                pltpu.VMEM((fields, hp, wp), jnp.float32),
                pltpu.VMEM((hp, wp), jnp.float32),
            ],
        ),
        out_shape=jax.ShapeDtypeStruct(adjoint.shape, jnp.float32),
        compiler_params=pltpu.CompilerParams(vmem_limit_bytes=60 * 1024 * 1024),
    )(where, weight, adjoint, land_mask, diffusivity, rows5, cols5, coriolis.reshape(h, 1), values, traj3)


def fold_rows(top_msg, fold_partner, width):
    lon_count = lax.axis_size("lon")
    lat_count = lax.axis_size("lat")
    lon = lax.axis_index("lon")
    nx = lon_count * width
    first = lon * width
    offset = (fold_partner[0] + first - (nx - 1)) % nx
    shift_tiles = offset // width
    shift_in = offset % width
    top = lat_count - 1

    def branch(q):
        def run(msg):
            pairs_a, pairs_b = [], []
            for t in range(lon_count):
                src_a = (lon_count - 1 - t + q) % lon_count
                src_b = (src_a + 1) % lon_count
                pairs_a.append((src_a * lat_count + top, t * lat_count + top))
                pairs_b.append((src_b * lat_count + top, t * lat_count + top))
            got_a = lax.ppermute(msg, ("lon", "lat"), pairs_a)
            got_b = lax.ppermute(msg, ("lon", "lat"), pairs_b)
            return jnp.concatenate([got_a, got_b], axis=2)

        return run

    both = lax.switch(shift_tiles, [branch(q) for q in range(lon_count)], top_msg)
    source = lax.broadcasted_iota(jnp.int32, (2 * width, width), 0)
    target = lax.broadcasted_iota(jnp.int32, (2 * width, width), 1)
    pick = source == width - 1 - target + shift_in
    return exact_pick("nmc,cl->nml", both, pick)


def per_device(
    adjoint,
    trajectory,
    diffusivity,
    land_mask,
    coriolis,
    obs_values,
    obs_weight,
    obs_owner,
    obs_offset,
    fold_partner,
):
    fields, levels, h, w = adjoint.shape
    lat_count = lax.axis_size("lat")
    lon_count = lax.axis_size("lon")
    lat = lax.axis_index("lat")
    n_work = fields * levels
    sign = jnp.array([1.0, 1.0, -1.0, -1.0], jnp.float32).reshape(fields, 1, 1, 1)

    def edge(rows):
        wet_rows = land_mask[:, rows, :].astype(jnp.float32)
        work_rows = adjoint[:, :, rows, :] * wet_rows[None]
        return work_rows, diffusivity[:, rows, :]

    top_work, top_diff = edge(slice(h - HALO, h))
    bot_work, bot_diff = edge(slice(0, HALO))
    top_msg = jnp.concatenate([top_work.reshape(n_work, HALO, w), top_diff], axis=0)
    bot_msg = jnp.concatenate([bot_work.reshape(n_work, HALO, w), bot_diff], axis=0)
    up = [(i, i + 1) for i in range(lat_count - 1)]
    down = [(i + 1, i) for i in range(lat_count - 1)]
    from_below = lax.ppermute(top_msg, "lat", up)
    from_above = lax.ppermute(bot_msg, "lat", down)
    signed_top = jnp.concatenate(
        [(top_work * sign).reshape(n_work, HALO, w), top_diff], axis=0
    )
    signed_top = jnp.concatenate(
        [signed_top[:, HALO - 1 - m : HALO - m, :] for m in range(HALO)], axis=1
    )
    folded = fold_rows(signed_top, fold_partner, w)
    north = jnp.where(lat == lat_count - 1, folded, from_above)
    gap = jnp.zeros((n_work + levels, PAD_ROWS - 2 * HALO, w), jnp.float32)
    rows_all = jnp.concatenate([north, gap, from_below], axis=1)
    rows5 = rows_all.reshape(fields + 1, levels, PAD_ROWS, w)

    lane = lax.broadcasted_iota(jnp.int32, (PAD_LANES, PAD_ROWS), 0)
    slot = lax.broadcasted_iota(jnp.int32, (PAD_LANES, PAD_ROWS), 1)
    take_first = (slot < HALO) & (lane == slot)
    take_last = (slot >= PAD_ROWS - HALO) & (lane == slot + PAD_LANES - PAD_ROWS)

    def edges(block):
        pick = lambda part, sel: exact_pick("nyx,xc->ncy", part, sel)
        return pick(block[..., :PAD_LANES], take_first) + pick(block[..., w - PAD_LANES :], take_last)

    wet_edges = edges(land_mask.astype(jnp.float32))
    adj_edges = edges(adjoint.reshape(n_work, h, w)).reshape(fields, levels, PAD_ROWS, h)
    work_edges = (adj_edges * wet_edges[None]).reshape(n_work, PAD_ROWS, h)
    interior = jnp.concatenate([work_edges, edges(diffusivity)], axis=0)
    col_msg = jnp.concatenate([interior, edges(rows_all)], axis=2)
    ring_west = [(i, (i - 1) % lon_count) for i in range(lon_count)]
    ring_east = [(i, (i + 1) % lon_count) for i in range(lon_count)]
    from_east = lax.ppermute(col_msg, "lon", ring_west)
    from_west = lax.ppermute(col_msg, "lon", ring_east)
    halo_slot = lax.broadcasted_iota(jnp.int32, col_msg.shape, 1)
    got_cols = jnp.where(halo_slot < HALO, from_east, from_west)
    place = (take_first | take_last).astype(jnp.float32).T
    cols5 = exact_pick("ncy,cl->nyl", got_cols, place)
    cols5 = cols5.reshape(fields + 1, levels, h + PAD_ROWS, PAD_LANES)


    devices = lon_count * lat_count
    seg_width = obs_values.shape[1]
    rows_sent = obs_values.shape[0]
    owner_index = obs_owner[:, 0]
    one_hot = (owner_index[:, None] == jnp.arange(devices, dtype=jnp.int32)[None, :]).astype(
        jnp.bfloat16
    )
    row_ids = jnp.arange(rows_sent, dtype=jnp.int32)
    before = (row_ids[None, :] < row_ids[:, None]).astype(jnp.bfloat16)
    earlier = lax.dot_general(
        before, one_hot, (((1,), (0,)), ((), ())), preferred_element_type=jnp.float32
    )
    slot_index = jnp.sum(earlier * one_hot.astype(jnp.float32), axis=1).astype(jnp.int32)
    dest_index = owner_index * CAP + slot_index
    slot_ids = jnp.arange(devices * CAP, dtype=jnp.int32)
    placement = (dest_index[:, None] == slot_ids[None, :]).astype(jnp.float32)
    send_values = exact_dot(placement, obs_values, 0).reshape(devices, CAP, seg_width)
    meta = jnp.stack([obs_weight, obs_offset.astype(jnp.float32)], axis=1)
    send_meta = exact_dot(placement, meta, 0).reshape(devices, CAP, 2)
    send_meta = jnp.swapaxes(send_meta, 1, 2).reshape(devices, 2 * CAP)
    send_meta = jnp.pad(send_meta, ((0, 0), (0, seg_width - 2 * CAP)))
    send = jnp.concatenate([send_values.reshape(devices, CAP * seg_width), send_meta], axis=1)
    got = lax.all_to_all(send, ("lon", "lat"), split_axis=0, concat_axis=0, tiled=True)
    got_values = got[:, : CAP * seg_width].reshape(devices * CAP, seg_width)
    got_meta = got[:, CAP * seg_width : CAP * seg_width + 2 * CAP].reshape(devices, 2, CAP)
    got_weight = got_meta[:, 0, :].reshape(devices * CAP)
    got_offset = got_meta[:, 1, :].reshape(devices * CAP).astype(jnp.int32)

    segments = w // seg_width
    seg_local = got_offset % segments
    rest = got_offset // segments
    row_local = rest % h
    layer = rest // h
    where = jnp.stack(
        [
            layer,
            row_local // 8 * 8,
            seg_local * seg_width,
            layer % levels,
            row_local % 8,
            layer // levels,
        ],
        axis=0,
    )
    return step_call(
        where,
        got_weight,
        adjoint,
        land_mask,
        diffusivity,
        rows5,
        cols5,
        coriolis,
        got_values,
        trajectory.reshape(n_work, h, w),
    )


def solution(mesh):
    return jax.shard_map(
        per_device,
        mesh=mesh,
        in_specs=(
            P(None, None, "lat", "lon"),
            P(None, None, "lat", "lon"),
            P(None, "lat", "lon"),
            P(None, "lat", "lon"),
            P("lat"),
            P(("lon", "lat"), None),
            P(("lon", "lat")),
            P(("lon", "lat"), None),
            P(("lon", "lat")),
            P("lon"),
        ),
        out_specs=P(None, None, "lat", "lon"),
        check_vma=False,
    )
```

```python
import jax
import jax.numpy as jnp
from jax import lax
from jax.experimental import pallas as pl
from jax.experimental.pallas import tpu as pltpu
from jax.sharding import PartitionSpec as P

NSUB = 3
CAP = 8
HALO = 3
PAD_ROWS = 8
PAD_LANES = 128


def exact_dot(left, right, left_dim):
    return lax.dot_general(
        left,
        right,
        (((left_dim,), (0,)), ((), ())),
        precision=lax.Precision.HIGHEST,
        preferred_element_type=jnp.float32,
    )


def step_kernel(
    where_ref, weight_ref, adj_ref, mask_ref, diff_ref, rows_ref, cols_ref, cor_ref, vals_ref,
    traj_ref, out_ref, xs, ds
):
    fields = adj_ref.shape[0]
    h, w = adj_ref.shape[2], adj_ref.shape[3]
    hp, wp = xs.shape[1], xs.shape[2]
    k = pl.program_id(0)
    per_step = vals_ref.shape[0] // pl.num_programs(0)

    @pl.when(k == 0)
    def _():
        out_ref[...] = jnp.zeros(out_ref.shape, jnp.float32)

    add_forcing(k * per_step, per_step, where_ref, weight_ref, vals_ref, traj_ref, mask_ref, out_ref)

    wet = mask_ref[k].astype(jnp.float32)
    for f in range(fields):
        xs[f, 0:h, 0:w] = adj_ref[f, 0] * wet
        xs[f, h:hp, 0:w] = rows_ref[f, 0]
        xs[f, :, w:wp] = cols_ref[f, 0]
    ds[0:h, 0:w] = diff_ref[0]
    ds[h:hp, 0:w] = rows_ref[fields, 0]
    ds[:, w:wp] = cols_ref[fields, 0]
    d = ds[...]
    done = []
    for f in range(fields):
        x = xs[f]
        for _ in range(NSUB):
            east = pltpu.roll(x, wp - 1, 1)
            west = pltpu.roll(x, 1, 1)
            north = pltpu.roll(x, hp - 1, 0)
            south = pltpu.roll(x, 1, 0)
            x = x + d * (east + west + north + south - 4.0 * x)
        done.append(x[0:h, 0:w])
    rot = cor_ref[...]
    out_ref[0, k] = out_ref[0, k] + wet * done[0]
    out_ref[1, k] = out_ref[1, k] + wet * done[1]
    out_ref[2, k] = out_ref[2, k] + wet * (done[2] - rot * done[3])
    out_ref[3, k] = out_ref[3, k] + wet * (done[3] + rot * done[2])


def add_forcing(start, count, where_ref, weight_ref, vals_ref, traj_ref, mask_ref, out_ref):
    seg_width = vals_ref.shape[1]
    sub = lax.broadcasted_iota(jnp.int32, (8, seg_width), 0)

    def add_row(i, value):
        layer = where_ref[0, i]
        rows = pl.ds(pl.multiple_of(where_ref[1, i], 8), 8)
        cols = pl.ds(pl.multiple_of(where_ref[2, i], seg_width), seg_width)
        level = where_ref[3, i]
        field = where_ref[5, i]
        sampled = traj_ref[layer, rows, cols]
        misfit = weight_ref[i] * (sampled - value)
        wet = mask_ref[level, rows, cols].astype(jnp.float32)
        hit = sub == where_ref[4, i]
        cur = out_ref[field, level, rows, cols]
        out_ref[field, level, rows, cols] = cur + jnp.where(hit, wet * misfit, 0.0)

    for t in range(count // 8):
        first = pl.multiple_of(start + 8 * t, 8)
        vals8 = vals_ref[pl.ds(first, 8), :]
        for j in range(8):
            add_row(first + j, vals8[j : j + 1, :])


def step_call(where, weight, adjoint, land_mask, diffusivity, rows5, cols5, coriolis, values, traj3):
    fields, levels, h, w = adjoint.shape
    hp, wp = h + PAD_ROWS, w + PAD_LANES
    rows_in = values.shape[0]
    per_step = -(-(-(-rows_in // levels)) // 8) * 8
    extra = per_step * levels - rows_in
    values = jnp.pad(values, ((0, extra), (0, 0)))
    weight = jnp.pad(weight, (0, extra))
    where = jnp.pad(where, ((0, 0), (0, extra)))
    whole = lambda shape: pl.BlockSpec(shape, lambda k, *_: (0,) * len(shape))
    return pl.pallas_call(
        step_kernel,
        grid_spec=pltpu.PrefetchScalarGridSpec(
            num_scalar_prefetch=2,
            grid=(levels,),
            in_specs=[
                pl.BlockSpec((fields, 1, h, w), lambda k, *_: (0, k, 0, 0)),
                whole(land_mask.shape),
                pl.BlockSpec((1, h, w), lambda k, *_: (k, 0, 0)),
                pl.BlockSpec((fields + 1, 1, PAD_ROWS, w), lambda k, *_: (0, k, 0, 0)),
                pl.BlockSpec((fields + 1, 1, hp, PAD_LANES), lambda k, *_: (0, k, 0, 0)),
                whole((h, 1)),
                whole(values.shape),
                whole(traj3.shape),
            ],
            out_specs=whole(adjoint.shape),
            scratch_shapes=[
                pltpu.VMEM((fields, hp, wp), jnp.float32),
                pltpu.VMEM((hp, wp), jnp.float32),
            ],
        ),
        out_shape=jax.ShapeDtypeStruct(adjoint.shape, jnp.float32),
        compiler_params=pltpu.CompilerParams(vmem_limit_bytes=60 * 1024 * 1024),
    )(where, weight, adjoint, land_mask, diffusivity, rows5, cols5, coriolis.reshape(h, 1), values, traj3)


def fold_rows(top_msg, fold_partner, width):
    lon_count = lax.axis_size("lon")
    lat_count = lax.axis_size("lat")
    lon = lax.axis_index("lon")
    nx = lon_count * width
    first = lon * width
    offset = (fold_partner[0] + first - (nx - 1)) % nx
    shift_tiles = offset // width
    shift_in = offset % width
    top = lat_count - 1

    def branch(q):
        def run(msg):
            pairs_a, pairs_b = [], []
            for t in range(lon_count):
                src_a = (lon_count - 1 - t + q) % lon_count
                src_b = (src_a + 1) % lon_count
                pairs_a.append((src_a * lat_count + top, t * lat_count + top))
                pairs_b.append((src_b * lat_count + top, t * lat_count + top))
            got_a = lax.ppermute(msg, ("lon", "lat"), pairs_a)
            got_b = lax.ppermute(msg, ("lon", "lat"), pairs_b)
            return jnp.concatenate([got_a, got_b], axis=2)

        return run

    both = lax.switch(shift_tiles, [branch(q) for q in range(lon_count)], top_msg)
    source = lax.broadcasted_iota(jnp.int32, (2 * width, width), 0)
    target = lax.broadcasted_iota(jnp.int32, (2 * width, width), 1)
    pick = (source == width - 1 - target + shift_in).astype(jnp.float32)
    return exact_dot(both, pick, 2)


def per_device(
    adjoint,
    trajectory,
    diffusivity,
    land_mask,
    coriolis,
    obs_values,
    obs_weight,
    obs_owner,
    obs_offset,
    fold_partner,
):
    fields, levels, h, w = adjoint.shape
    lat_count = lax.axis_size("lat")
    lon_count = lax.axis_size("lon")
    lat = lax.axis_index("lat")
    n_work = fields * levels
    sign = jnp.array([1.0, 1.0, -1.0, -1.0], jnp.float32).reshape(fields, 1, 1, 1)

    def edge(rows):
        wet_rows = land_mask[:, rows, :].astype(jnp.float32)
        work_rows = adjoint[:, :, rows, :] * wet_rows[None]
        return work_rows, diffusivity[:, rows, :]

    top_work, top_diff = edge(slice(h - HALO, h))
    bot_work, bot_diff = edge(slice(0, HALO))
    top_msg = jnp.concatenate([top_work.reshape(n_work, HALO, w), top_diff], axis=0)
    bot_msg = jnp.concatenate([bot_work.reshape(n_work, HALO, w), bot_diff], axis=0)
    up = [(i, i + 1) for i in range(lat_count - 1)]
    down = [(i + 1, i) for i in range(lat_count - 1)]
    from_below = lax.ppermute(top_msg, "lat", up)
    from_above = lax.ppermute(bot_msg, "lat", down)
    signed_top = jnp.concatenate(
        [(top_work * sign).reshape(n_work, HALO, w), top_diff], axis=0
    )
    signed_top = jnp.concatenate(
        [signed_top[:, HALO - 1 - m : HALO - m, :] for m in range(HALO)], axis=1
    )
    folded = fold_rows(signed_top, fold_partner, w)
    north = jnp.where(lat == lat_count - 1, folded, from_above)
    gap = jnp.zeros((n_work + levels, PAD_ROWS - 2 * HALO, w), jnp.float32)
    rows_all = jnp.concatenate([north, gap, from_below], axis=1)
    rows5 = rows_all.reshape(fields + 1, levels, PAD_ROWS, w)

    lane = lax.broadcasted_iota(jnp.int32, (PAD_LANES, PAD_ROWS), 0)
    slot = lax.broadcasted_iota(jnp.int32, (PAD_LANES, PAD_ROWS), 1)
    take_first = (slot < HALO) & (lane == slot)
    take_last = (slot >= PAD_ROWS - HALO) & (lane == slot + PAD_LANES - PAD_ROWS)

    def edges(block):
        pick = lambda part, sel: jnp.einsum(
            "nyx,xc->ncy", part, sel.astype(jnp.float32), precision=lax.Precision.HIGHEST
        )
        return pick(block[..., :PAD_LANES], take_first) + pick(block[..., w - PAD_LANES :], take_last)

    def end_tiles(lanes):
        work = adjoint[..., lanes] * land_mask[None, ..., lanes].astype(jnp.float32)
        return jnp.concatenate([work.reshape(n_work, h, PAD_LANES), diffusivity[..., lanes]], axis=0)

    interior = jnp.einsum(
        "nyx,xc->ncy",
        end_tiles(slice(0, PAD_LANES)),
        take_first.astype(jnp.float32),
        precision=lax.Precision.HIGHEST,
    ) + jnp.einsum(
        "nyx,xc->ncy",
        end_tiles(slice(w - PAD_LANES, w)),
        take_last.astype(jnp.float32),
        precision=lax.Precision.HIGHEST,
    )
    col_msg = jnp.concatenate([interior, edges(rows_all)], axis=2)
    ring_west = [(i, (i - 1) % lon_count) for i in range(lon_count)]
    ring_east = [(i, (i + 1) % lon_count) for i in range(lon_count)]
    from_east = lax.ppermute(col_msg, "lon", ring_west)
    from_west = lax.ppermute(col_msg, "lon", ring_east)
    halo_slot = lax.broadcasted_iota(jnp.int32, col_msg.shape, 1)
    got_cols = jnp.where(halo_slot < HALO, from_east, from_west)
    place = (take_first | take_last).astype(jnp.float32).T
    cols5 = jnp.einsum("ncy,cl->nyl", got_cols, place, precision=lax.Precision.HIGHEST)
    cols5 = cols5.reshape(fields + 1, levels, h + PAD_ROWS, PAD_LANES)


    devices = lon_count * lat_count
    seg_width = obs_values.shape[1]
    rows_sent = obs_values.shape[0]
    owner_index = obs_owner[:, 0]
    one_hot = (owner_index[:, None] == jnp.arange(devices, dtype=jnp.int32)[None, :]).astype(
        jnp.bfloat16
    )
    row_ids = jnp.arange(rows_sent, dtype=jnp.int32)
    before = (row_ids[None, :] < row_ids[:, None]).astype(jnp.bfloat16)
    earlier = lax.dot_general(
        before, one_hot, (((1,), (0,)), ((), ())), preferred_element_type=jnp.float32
    )
    slot_index = jnp.sum(earlier * one_hot.astype(jnp.float32), axis=1).astype(jnp.int32)
    dest_index = owner_index * CAP + slot_index
    slot_ids = jnp.arange(devices * CAP, dtype=jnp.int32)
    placement = (dest_index[:, None] == slot_ids[None, :]).astype(jnp.float32)
    send_values = exact_dot(placement, obs_values, 0).reshape(devices, CAP, seg_width)
    meta = jnp.stack([obs_weight, obs_offset.astype(jnp.float32)], axis=1)
    send_meta = exact_dot(placement, meta, 0).reshape(devices, CAP, 2)
    send_meta = jnp.swapaxes(send_meta, 1, 2).reshape(devices, 2 * CAP)
    send_meta = jnp.pad(send_meta, ((0, 0), (0, seg_width - 2 * CAP)))
    send = jnp.concatenate([send_values.reshape(devices, CAP * seg_width), send_meta], axis=1)
    got = lax.all_to_all(send, ("lon", "lat"), split_axis=0, concat_axis=0, tiled=True)
    got_values = got[:, : CAP * seg_width].reshape(devices * CAP, seg_width)
    got_meta = got[:, CAP * seg_width : CAP * seg_width + 2 * CAP].reshape(devices, 2, CAP)
    got_weight = got_meta[:, 0, :].reshape(devices * CAP)
    got_offset = got_meta[:, 1, :].reshape(devices * CAP).astype(jnp.int32)

    segments = w // seg_width
    seg_local = got_offset % segments
    rest = got_offset // segments
    row_local = rest % h
    layer = rest // h
    where = jnp.stack(
        [
            layer,
            row_local // 8 * 8,
            seg_local * seg_width,
            layer % levels,
            row_local % 8,
            layer // levels,
        ],
        axis=0,
    )
    return step_call(
        where,
        got_weight,
        adjoint,
        land_mask,
        diffusivity,
        rows5,
        cols5,
        coriolis,
        got_values,
        trajectory.reshape(n_work, h, w),
    )


def solution(mesh):
    return jax.shard_map(
        per_device,
        mesh=mesh,
        in_specs=(
            P(None, None, "lat", "lon"),
            P(None, None, "lat", "lon"),
            P(None, "lat", "lon"),
            P(None, "lat", "lon"),
            P("lat"),
            P(("lon", "lat"), None),
            P(("lon", "lat")),
            P(("lon", "lat"), None),
            P(("lon", "lat")),
            P("lon"),
        ),
        out_specs=P(None, None, "lat", "lon"),
        check_vma=False,
    )
```

```python
import jax
import jax.numpy as jnp
from jax import lax
from jax.experimental import pallas as pl
from jax.experimental.pallas import tpu as pltpu
from jax.sharding import PartitionSpec as P

NSUB = 3
CAP = 8
HALO = 3
PAD_ROWS = 8
PAD_LANES = 128


def exact_dot(left, right, left_dim):
    return lax.dot_general(
        left,
        right,
        (((left_dim,), (0,)), ((), ())),
        precision=lax.Precision.HIGHEST,
        preferred_element_type=jnp.float32,
    )


def step_kernel(
    where_ref, weight_ref, adj_ref, mask_ref, diff_ref, rows_ref, cols_ref, cor_ref, vals_ref,
    traj_ref, out_ref, xs, ds
):
    fields = adj_ref.shape[0]
    h, w = adj_ref.shape[2], adj_ref.shape[3]
    hp, wp = xs.shape[1], xs.shape[2]
    k = pl.program_id(0)
    per_step = vals_ref.shape[0] // pl.num_programs(0)

    @pl.when(k == 0)
    def _():
        out_ref[...] = jnp.zeros(out_ref.shape, jnp.float32)

    add_forcing(k * per_step, per_step, where_ref, weight_ref, vals_ref, traj_ref, mask_ref, out_ref)

    wet = mask_ref[k].astype(jnp.float32)
    for f in range(fields):
        xs[f, 0:h, 0:w] = adj_ref[f, 0] * wet
        xs[f, h:hp, 0:w] = rows_ref[f, 0]
        xs[f, :, w:wp] = cols_ref[f, 0]
    ds[0:h, 0:w] = diff_ref[0]
    ds[h:hp, 0:w] = rows_ref[fields, 0]
    ds[:, w:wp] = cols_ref[fields, 0]
    d = ds[...]
    done = []
    for f in range(fields):
        x = xs[f]
        for _ in range(NSUB):
            east = pltpu.roll(x, wp - 1, 1)
            west = pltpu.roll(x, 1, 1)
            north = pltpu.roll(x, hp - 1, 0)
            south = pltpu.roll(x, 1, 0)
            x = x + d * (east + west + north + south - 4.0 * x)
        done.append(x[0:h, 0:w])
    rot = cor_ref[...]
    out_ref[0, k] = out_ref[0, k] + wet * done[0]
    out_ref[1, k] = out_ref[1, k] + wet * done[1]
    out_ref[2, k] = out_ref[2, k] + wet * (done[2] - rot * done[3])
    out_ref[3, k] = out_ref[3, k] + wet * (done[3] + rot * done[2])


def add_forcing(start, count, where_ref, weight_ref, vals_ref, traj_ref, mask_ref, out_ref):
    seg_width = vals_ref.shape[1]
    sub = lax.broadcasted_iota(jnp.int32, (8, seg_width), 0)

    def add_row(i, value):
        layer = where_ref[0, i]
        rows = pl.ds(pl.multiple_of(where_ref[1, i], 8), 8)
        cols = pl.ds(pl.multiple_of(where_ref[2, i], seg_width), seg_width)
        level = where_ref[3, i]
        field = where_ref[5, i]
        sampled = traj_ref[layer, rows, cols]
        misfit = weight_ref[i] * (sampled - value)
        wet = mask_ref[level, rows, cols].astype(jnp.float32)
        hit = sub == where_ref[4, i]
        cur = out_ref[field, level, rows, cols]
        out_ref[field, level, rows, cols] = cur + jnp.where(hit, wet * misfit, 0.0)

    for t in range(count // 8):
        first = pl.multiple_of(start + 8 * t, 8)
        vals8 = vals_ref[pl.ds(first, 8), :]
        for j in range(8):
            add_row(first + j, vals8[j : j + 1, :])


def step_call(where, weight, adjoint, land_mask, diffusivity, rows5, cols5, coriolis, values, traj3):
    fields, levels, h, w = adjoint.shape
    hp, wp = h + PAD_ROWS, w + PAD_LANES
    rows_in = values.shape[0]
    per_step = -(-(-(-rows_in // levels)) // 8) * 8
    extra = per_step * levels - rows_in
    values = jnp.pad(values, ((0, extra), (0, 0)))
    weight = jnp.pad(weight, (0, extra))
    where = jnp.pad(where, ((0, 0), (0, extra)))
    whole = lambda shape: pl.BlockSpec(shape, lambda k, *_: (0,) * len(shape))
    return pl.pallas_call(
        step_kernel,
        grid_spec=pltpu.PrefetchScalarGridSpec(
            num_scalar_prefetch=2,
            grid=(levels,),
            in_specs=[
                pl.BlockSpec((fields, 1, h, w), lambda k, *_: (0, k, 0, 0)),
                whole(land_mask.shape),
                pl.BlockSpec((1, h, w), lambda k, *_: (k, 0, 0)),
                pl.BlockSpec((fields + 1, 1, PAD_ROWS, w), lambda k, *_: (0, k, 0, 0)),
                pl.BlockSpec((fields + 1, 1, hp, PAD_LANES), lambda k, *_: (0, k, 0, 0)),
                whole((h, 1)),
                whole(values.shape),
                whole(traj3.shape),
            ],
            out_specs=whole(adjoint.shape),
            scratch_shapes=[
                pltpu.VMEM((fields, hp, wp), jnp.float32),
                pltpu.VMEM((hp, wp), jnp.float32),
            ],
        ),
        out_shape=jax.ShapeDtypeStruct(adjoint.shape, jnp.float32),
        compiler_params=pltpu.CompilerParams(vmem_limit_bytes=60 * 1024 * 1024),
    )(where, weight, adjoint, land_mask, diffusivity, rows5, cols5, coriolis.reshape(h, 1), values, traj3)


def fold_rows(top_msg, fold_partner, width):
    lon_count = lax.axis_size("lon")
    lat_count = lax.axis_size("lat")
    lon = lax.axis_index("lon")
    nx = lon_count * width
    first = lon * width
    offset = (fold_partner[0] + first - (nx - 1)) % nx
    shift_tiles = offset // width
    shift_in = offset % width
    top = lat_count - 1

    def branch(q):
        def run(msg):
            pairs_a, pairs_b = [], []
            for t in range(lon_count):
                src_a = (lon_count - 1 - t + q) % lon_count
                src_b = (src_a + 1) % lon_count
                pairs_a.append((src_a * lat_count + top, t * lat_count + top))
                pairs_b.append((src_b * lat_count + top, t * lat_count + top))
            got_a = lax.ppermute(msg, ("lon", "lat"), pairs_a)
            got_b = lax.ppermute(msg, ("lon", "lat"), pairs_b)
            return jnp.concatenate([got_a, got_b], axis=2)

        return run

    both = lax.switch(shift_tiles, [branch(q) for q in range(lon_count)], top_msg)
    source = lax.broadcasted_iota(jnp.int32, (2 * width, width), 0)
    target = lax.broadcasted_iota(jnp.int32, (2 * width, width), 1)
    pick = (source == width - 1 - target + shift_in).astype(jnp.float32)
    return exact_dot(both, pick, 2)


def per_device(
    adjoint,
    trajectory,
    diffusivity,
    land_mask,
    coriolis,
    obs_values,
    obs_weight,
    obs_owner,
    obs_offset,
    fold_partner,
):
    fields, levels, h, w = adjoint.shape
    lat_count = lax.axis_size("lat")
    lon_count = lax.axis_size("lon")
    lat = lax.axis_index("lat")
    n_work = fields * levels
    sign = jnp.array([1.0, 1.0, -1.0, -1.0], jnp.float32).reshape(fields, 1, 1, 1)

    def edge(rows):
        wet_rows = land_mask[:, rows, :].astype(jnp.float32)
        work_rows = adjoint[:, :, rows, :] * wet_rows[None]
        return work_rows, diffusivity[:, rows, :]

    top_work, top_diff = edge(slice(h - HALO, h))
    bot_work, bot_diff = edge(slice(0, HALO))
    top_msg = jnp.concatenate([top_work.reshape(n_work, HALO, w), top_diff], axis=0)
    bot_msg = jnp.concatenate([bot_work.reshape(n_work, HALO, w), bot_diff], axis=0)
    up = [(i, i + 1) for i in range(lat_count - 1)]
    down = [(i + 1, i) for i in range(lat_count - 1)]
    from_below = lax.ppermute(top_msg, "lat", up)
    from_above = lax.ppermute(bot_msg, "lat", down)
    signed_top = jnp.concatenate(
        [(top_work * sign).reshape(n_work, HALO, w), top_diff], axis=0
    )
    signed_top = jnp.concatenate(
        [signed_top[:, HALO - 1 - m : HALO - m, :] for m in range(HALO)], axis=1
    )
    folded = fold_rows(signed_top, fold_partner, w)
    north = jnp.where(lat == lat_count - 1, folded, from_above)
    gap = jnp.zeros((n_work + levels, PAD_ROWS - 2 * HALO, w), jnp.float32)
    rows_all = jnp.concatenate([north, gap, from_below], axis=1)
    rows5 = rows_all.reshape(fields + 1, levels, PAD_ROWS, w)

    lane = lax.broadcasted_iota(jnp.int32, (PAD_LANES, PAD_ROWS), 0)
    slot = lax.broadcasted_iota(jnp.int32, (PAD_LANES, PAD_ROWS), 1)
    take_first = (slot < HALO) & (lane == slot)
    take_last = (slot >= PAD_ROWS - HALO) & (lane == slot + PAD_LANES - PAD_ROWS)

    def edges(block):
        pick = lambda part, sel: jnp.einsum(
            "nyx,xc->ncy", part, sel.astype(jnp.float32), precision=lax.Precision.HIGHEST
        )
        return pick(block[..., :PAD_LANES], take_first) + pick(block[..., w - PAD_LANES :], take_last)

    def end_tiles(lanes):
        work = adjoint[..., lanes] * land_mask[None, ..., lanes].astype(jnp.float32)
        return jnp.concatenate([work.reshape(n_work, h, PAD_LANES), diffusivity[..., lanes]], axis=0)

    interior = jnp.einsum(
        "nyx,xc->ncy",
        end_tiles(slice(0, PAD_LANES)),
        take_first.astype(jnp.float32),
        precision=lax.Precision.HIGHEST,
    ) + jnp.einsum(
        "nyx,xc->ncy",
        end_tiles(slice(w - PAD_LANES, w)),
        take_last.astype(jnp.float32),
        precision=lax.Precision.HIGHEST,
    )
    col_msg = jnp.concatenate([interior, edges(rows_all)], axis=2)
    ring_west = [(i, (i - 1) % lon_count) for i in range(lon_count)]
    ring_east = [(i, (i + 1) % lon_count) for i in range(lon_count)]
    from_east = lax.ppermute(col_msg, "lon", ring_west)
    from_west = lax.ppermute(col_msg, "lon", ring_east)
    halo_slot = lax.broadcasted_iota(jnp.int32, col_msg.shape, 1)
    got_cols = jnp.where(halo_slot < HALO, from_east, from_west)
    place = (take_first | take_last).astype(jnp.float32).T
    cols5 = jnp.einsum("ncy,cl->nyl", got_cols, place, precision=lax.Precision.HIGHEST)
    cols5 = cols5.reshape(fields + 1, levels, h + PAD_ROWS, PAD_LANES)


    devices = lon_count * lat_count
    seg_width = obs_values.shape[1]
    rows_sent = obs_values.shape[0]
    owner_index = obs_owner[:, 0]
    one_hot = (owner_index[:, None] == jnp.arange(devices, dtype=jnp.int32)[None, :]).astype(
        jnp.bfloat16
    )
    row_ids = jnp.arange(rows_sent, dtype=jnp.int32)
    before = (row_ids[None, :] < row_ids[:, None]).astype(jnp.bfloat16)
    earlier = lax.dot_general(
        before, one_hot, (((1,), (0,)), ((), ())), preferred_element_type=jnp.float32
    )
    slot_index = jnp.sum(earlier * one_hot.astype(jnp.float32), axis=1).astype(jnp.int32)
    dest_index = owner_index * CAP + slot_index
    slot_ids = jnp.arange(devices * CAP, dtype=jnp.int32)
    placement = (dest_index[:, None] == slot_ids[None, :]).astype(jnp.float32)
    meta = jnp.stack([obs_weight, obs_offset.astype(jnp.float32)], axis=1)
    placed = exact_dot(placement, jnp.concatenate([obs_values, meta], axis=1), 0)
    send_values = placed[:, :seg_width].reshape(devices, CAP, seg_width)
    send_meta = placed[:, seg_width:].reshape(devices, CAP, 2)
    send_meta = jnp.swapaxes(send_meta, 1, 2).reshape(devices, 2 * CAP)
    send_meta = jnp.pad(send_meta, ((0, 0), (0, seg_width - 2 * CAP)))
    send = jnp.concatenate([send_values.reshape(devices, CAP * seg_width), send_meta], axis=1)
    got = lax.all_to_all(send, ("lon", "lat"), split_axis=0, concat_axis=0, tiled=True)
    got_values = got[:, : CAP * seg_width].reshape(devices * CAP, seg_width)
    got_meta = got[:, CAP * seg_width : CAP * seg_width + 2 * CAP].reshape(devices, 2, CAP)
    got_weight = got_meta[:, 0, :].reshape(devices * CAP)
    got_offset = got_meta[:, 1, :].reshape(devices * CAP).astype(jnp.int32)

    segments = w // seg_width
    seg_local = got_offset % segments
    rest = got_offset // segments
    row_local = rest % h
    layer = rest // h
    where = jnp.stack(
        [
            layer,
            row_local // 8 * 8,
            seg_local * seg_width,
            layer % levels,
            row_local % 8,
            layer // levels,
        ],
        axis=0,
    )
    return step_call(
        where,
        got_weight,
        adjoint,
        land_mask,
        diffusivity,
        rows5,
        cols5,
        coriolis,
        got_values,
        trajectory.reshape(n_work, h, w),
    )


def solution(mesh):
    return jax.shard_map(
        per_device,
        mesh=mesh,
        in_specs=(
            P(None, None, "lat", "lon"),
            P(None, None, "lat", "lon"),
            P(None, "lat", "lon"),
            P(None, "lat", "lon"),
            P("lat"),
            P(("lon", "lat"), None),
            P(("lon", "lat")),
            P(("lon", "lat"), None),
            P(("lon", "lat")),
            P("lon"),
        ),
        out_specs=P(None, None, "lat", "lon"),
        check_vma=False,
    )
```

```python
import jax
import jax.numpy as jnp
from jax import lax
from jax.experimental import pallas as pl
from jax.experimental.pallas import tpu as pltpu
from jax.sharding import PartitionSpec as P

NSUB = 3
CAP = 8
HALO = 3
PAD_ROWS = 8
PAD_LANES = 128


def exact_dot(left, right, left_dim):
    return lax.dot_general(
        left,
        right,
        (((left_dim,), (0,)), ((), ())),
        precision=lax.Precision.HIGHEST,
        preferred_element_type=jnp.float32,
    )


def step_kernel(
    where_ref, weight_ref, adj_ref, mask_ref, diff_ref, rows_ref, cols_ref, cor_ref, vals_ref,
    traj_ref, out_ref, xs, ds
):
    fields = adj_ref.shape[0]
    h, w = adj_ref.shape[2], adj_ref.shape[3]
    hp, wp = xs.shape[1], xs.shape[2]
    k = pl.program_id(0)
    per_step = vals_ref.shape[0] // pl.num_programs(0)

    @pl.when(k == 0)
    def _():
        out_ref[...] = jnp.zeros(out_ref.shape, jnp.float32)

    add_forcing(k * per_step, per_step, where_ref, weight_ref, vals_ref, traj_ref, mask_ref, out_ref)

    wet = mask_ref[k].astype(jnp.float32)
    for f in range(fields):
        xs[f, 0:h, 0:w] = adj_ref[f, 0] * wet
        xs[f, h:hp, 0:w] = rows_ref[f, 0]
        xs[f, :, w:wp] = cols_ref[f, 0]
    ds[0:h, 0:w] = diff_ref[0]
    ds[h:hp, 0:w] = rows_ref[fields, 0]
    ds[:, w:wp] = cols_ref[fields, 0]
    d = ds[...]
    done = []
    for f in range(fields):
        x = xs[f]
        for _ in range(NSUB):
            east = pltpu.roll(x, wp - 1, 1)
            west = pltpu.roll(x, 1, 1)
            north = pltpu.roll(x, hp - 1, 0)
            south = pltpu.roll(x, 1, 0)
            x = x + d * (east + west + north + south - 4.0 * x)
        done.append(x[0:h, 0:w])
    rot = cor_ref[...]
    out_ref[0, k] = out_ref[0, k] + wet * done[0]
    out_ref[1, k] = out_ref[1, k] + wet * done[1]
    out_ref[2, k] = out_ref[2, k] + wet * (done[2] - rot * done[3])
    out_ref[3, k] = out_ref[3, k] + wet * (done[3] + rot * done[2])


def add_forcing(start, count, where_ref, weight_ref, vals_ref, traj_ref, mask_ref, out_ref):
    seg_width = vals_ref.shape[1]
    sub = lax.broadcasted_iota(jnp.int32, (8, seg_width), 0)

    def add_row(i, value):
        layer = where_ref[0, i]
        rows = pl.ds(pl.multiple_of(where_ref[1, i], 8), 8)
        cols = pl.ds(pl.multiple_of(where_ref[2, i], seg_width), seg_width)
        level = where_ref[3, i]
        field = where_ref[5, i]
        sampled = traj_ref[layer, rows, cols]
        misfit = weight_ref[i] * (sampled - value)
        wet = mask_ref[level, rows, cols].astype(jnp.float32)
        hit = sub == where_ref[4, i]
        cur = out_ref[field, level, rows, cols]
        out_ref[field, level, rows, cols] = cur + jnp.where(hit, wet * misfit, 0.0)

    for t in range(count // 8):
        first = pl.multiple_of(start + 8 * t, 8)
        vals8 = vals_ref[pl.ds(first, 8), :]
        for j in range(8):
            add_row(first + j, vals8[j : j + 1, :])


def step_call(where, weight, adjoint, land_mask, diffusivity, rows5, cols5, coriolis, values, traj3):
    fields, levels, h, w = adjoint.shape
    hp, wp = h + PAD_ROWS, w + PAD_LANES
    rows_in = values.shape[0]
    per_step = -(-(-(-rows_in // levels)) // 8) * 8
    extra = per_step * levels - rows_in
    values = jnp.pad(values, ((0, extra), (0, 0)))
    weight = jnp.pad(weight, (0, extra))
    where = jnp.pad(where, ((0, 0), (0, extra)))
    whole = lambda shape: pl.BlockSpec(shape, lambda k, *_: (0,) * len(shape))
    return pl.pallas_call(
        step_kernel,
        grid_spec=pltpu.PrefetchScalarGridSpec(
            num_scalar_prefetch=2,
            grid=(levels,),
            in_specs=[
                pl.BlockSpec((fields, 1, h, w), lambda k, *_: (0, k, 0, 0)),
                whole(land_mask.shape),
                pl.BlockSpec((1, h, w), lambda k, *_: (k, 0, 0)),
                pl.BlockSpec((fields + 1, 1, PAD_ROWS, w), lambda k, *_: (0, k, 0, 0)),
                pl.BlockSpec((fields + 1, 1, hp, PAD_LANES), lambda k, *_: (0, k, 0, 0)),
                whole((h, 1)),
                whole(values.shape),
                whole(traj3.shape),
            ],
            out_specs=whole(adjoint.shape),
            scratch_shapes=[
                pltpu.VMEM((fields, hp, wp), jnp.float32),
                pltpu.VMEM((hp, wp), jnp.float32),
            ],
        ),
        out_shape=jax.ShapeDtypeStruct(adjoint.shape, jnp.float32),
        compiler_params=pltpu.CompilerParams(vmem_limit_bytes=60 * 1024 * 1024),
    )(where, weight, adjoint, land_mask, diffusivity, rows5, cols5, coriolis.reshape(h, 1), values, traj3)


def fold_rows(top_msg, fold_partner, width):
    lon_count = lax.axis_size("lon")
    lat_count = lax.axis_size("lat")
    lon = lax.axis_index("lon")
    nx = lon_count * width
    first = lon * width
    offset = (fold_partner[0] + first - (nx - 1)) % nx
    shift_tiles = offset // width
    shift_in = offset % width
    top = lat_count - 1

    def branch(q):
        def run(msg):
            pairs_a, pairs_b = [], []
            for t in range(lon_count):
                src_a = (lon_count - 1 - t + q) % lon_count
                src_b = (src_a + 1) % lon_count
                pairs_a.append((src_a * lat_count + top, t * lat_count + top))
                pairs_b.append((src_b * lat_count + top, t * lat_count + top))
            got_a = lax.ppermute(msg, ("lon", "lat"), pairs_a)
            got_b = lax.ppermute(msg, ("lon", "lat"), pairs_b)
            return jnp.concatenate([got_a, got_b], axis=2)

        return run

    both = lax.switch(shift_tiles, [branch(q) for q in range(lon_count)], top_msg)
    source = lax.broadcasted_iota(jnp.int32, (2 * width, width), 0)
    target = lax.broadcasted_iota(jnp.int32, (2 * width, width), 1)
    pick = (source == width - 1 - target + shift_in).astype(jnp.float32)
    return exact_dot(both, pick, 2)


def per_device(
    adjoint,
    trajectory,
    diffusivity,
    land_mask,
    coriolis,
    obs_values,
    obs_weight,
    obs_owner,
    obs_offset,
    fold_partner,
):
    fields, levels, h, w = adjoint.shape
    lat_count = lax.axis_size("lat")
    lon_count = lax.axis_size("lon")
    lat = lax.axis_index("lat")
    n_work = fields * levels
    sign = jnp.array([1.0, 1.0, -1.0, -1.0], jnp.float32).reshape(fields, 1, 1, 1)

    def edge(rows):
        wet_rows = land_mask[:, rows, :].astype(jnp.float32)
        work_rows = adjoint[:, :, rows, :] * wet_rows[None]
        return work_rows, diffusivity[:, rows, :]

    top_work, top_diff = edge(slice(h - HALO, h))
    bot_work, bot_diff = edge(slice(0, HALO))
    top_msg = jnp.concatenate([top_work.reshape(n_work, HALO, w), top_diff], axis=0)
    bot_msg = jnp.concatenate([bot_work.reshape(n_work, HALO, w), bot_diff], axis=0)
    up = [(i, i + 1) for i in range(lat_count - 1)]
    down = [(i + 1, i) for i in range(lat_count - 1)]
    from_below = lax.ppermute(top_msg, "lat", up)
    from_above = lax.ppermute(bot_msg, "lat", down)
    signed_top = jnp.concatenate(
        [(top_work * sign).reshape(n_work, HALO, w), top_diff], axis=0
    )
    signed_top = jnp.concatenate(
        [signed_top[:, HALO - 1 - m : HALO - m, :] for m in range(HALO)], axis=1
    )
    folded = fold_rows(signed_top, fold_partner, w)
    north = jnp.where(lat == lat_count - 1, folded, from_above)
    gap = jnp.zeros((n_work + levels, PAD_ROWS - 2 * HALO, w), jnp.float32)
    rows_all = jnp.concatenate([north, gap, from_below], axis=1)
    rows5 = rows_all.reshape(fields + 1, levels, PAD_ROWS, w)

    lane = lax.broadcasted_iota(jnp.int32, (PAD_LANES, PAD_ROWS), 0)
    slot = lax.broadcasted_iota(jnp.int32, (PAD_LANES, PAD_ROWS), 1)
    take_first = (slot < HALO) & (lane == slot)
    take_last = (slot >= PAD_ROWS - HALO) & (lane == slot + PAD_LANES - PAD_ROWS)

    def edges(block):
        pick = lambda part, sel: jnp.einsum(
            "nyx,xc->ncy", part, sel.astype(jnp.float32), precision=lax.Precision.HIGHEST
        )
        return pick(block[..., :PAD_LANES], take_first) + pick(block[..., w - PAD_LANES :], take_last)

    def end_tiles(lanes):
        work = adjoint[..., lanes] * land_mask[None, ..., lanes].astype(jnp.float32)
        return jnp.concatenate([work.reshape(n_work, h, PAD_LANES), diffusivity[..., lanes]], axis=0)

    interior = jnp.einsum(
        "nyx,xc->ncy",
        end_tiles(slice(0, PAD_LANES)),
        take_first.astype(jnp.float32),
        precision=lax.Precision.HIGHEST,
    ) + jnp.einsum(
        "nyx,xc->ncy",
        end_tiles(slice(w - PAD_LANES, w)),
        take_last.astype(jnp.float32),
        precision=lax.Precision.HIGHEST,
    )
    corner_gap = jnp.zeros((n_work + levels, PAD_ROWS, PAD_ROWS - 2 * HALO), jnp.float32)
    col_msg = jnp.concatenate([interior, edges(north), corner_gap, edges(from_below)], axis=2)
    ring_west = [(i, (i - 1) % lon_count) for i in range(lon_count)]
    ring_east = [(i, (i + 1) % lon_count) for i in range(lon_count)]
    from_east = lax.ppermute(col_msg, "lon", ring_west)
    from_west = lax.ppermute(col_msg, "lon", ring_east)
    halo_slot = lax.broadcasted_iota(jnp.int32, col_msg.shape, 1)
    got_cols = jnp.where(halo_slot < HALO, from_east, from_west)
    place = (take_first | take_last).astype(jnp.float32).T
    cols5 = jnp.einsum("ncy,cl->nyl", got_cols, place, precision=lax.Precision.HIGHEST)
    cols5 = cols5.reshape(fields + 1, levels, h + PAD_ROWS, PAD_LANES)


    devices = lon_count * lat_count
    seg_width = obs_values.shape[1]
    rows_sent = obs_values.shape[0]
    owner_index = obs_owner[:, 0]
    one_hot = (owner_index[:, None] == jnp.arange(devices, dtype=jnp.int32)[None, :]).astype(
        jnp.bfloat16
    )
    row_ids = jnp.arange(rows_sent, dtype=jnp.int32)
    before = (row_ids[None, :] < row_ids[:, None]).astype(jnp.bfloat16)
    earlier = lax.dot_general(
        before, one_hot, (((1,), (0,)), ((), ())), preferred_element_type=jnp.float32
    )
    slot_index = jnp.sum(earlier * one_hot.astype(jnp.float32), axis=1).astype(jnp.int32)
    dest_index = owner_index * CAP + slot_index
    slot_ids = jnp.arange(devices * CAP, dtype=jnp.int32)
    placement = (dest_index[:, None] == slot_ids[None, :]).astype(jnp.float32)
    meta = jnp.stack([obs_weight, obs_offset.astype(jnp.float32)], axis=1)
    placed = exact_dot(placement, jnp.concatenate([obs_values, meta], axis=1), 0)
    send_values = placed[:, :seg_width].reshape(devices, CAP, seg_width)
    send_meta = placed[:, seg_width:].reshape(devices, CAP, 2)
    send_meta = jnp.swapaxes(send_meta, 1, 2).reshape(devices, 2 * CAP)
    send_meta = jnp.pad(send_meta, ((0, 0), (0, seg_width - 2 * CAP)))
    send = jnp.concatenate([send_values.reshape(devices, CAP * seg_width), send_meta], axis=1)
    got = lax.all_to_all(send, ("lon", "lat"), split_axis=0, concat_axis=0, tiled=True)
    got_values = got[:, : CAP * seg_width].reshape(devices * CAP, seg_width)
    got_meta = got[:, CAP * seg_width : CAP * seg_width + 2 * CAP].reshape(devices, 2, CAP)
    got_weight = got_meta[:, 0, :].reshape(devices * CAP)
    got_offset = got_meta[:, 1, :].reshape(devices * CAP).astype(jnp.int32)

    segments = w // seg_width
    seg_local = got_offset % segments
    rest = got_offset // segments
    row_local = rest % h
    layer = rest // h
    where = jnp.stack(
        [
            layer,
            row_local // 8 * 8,
            seg_local * seg_width,
            layer % levels,
            row_local % 8,
            layer // levels,
        ],
        axis=0,
    )
    return step_call(
        where,
        got_weight,
        adjoint,
        land_mask,
        diffusivity,
        rows5,
        cols5,
        coriolis,
        got_values,
        trajectory.reshape(n_work, h, w),
    )


def solution(mesh):
    return jax.shard_map(
        per_device,
        mesh=mesh,
        in_specs=(
            P(None, None, "lat", "lon"),
            P(None, None, "lat", "lon"),
            P(None, "lat", "lon"),
            P(None, "lat", "lon"),
            P("lat"),
            P(("lon", "lat"), None),
            P(("lon", "lat")),
            P(("lon", "lat"), None),
            P(("lon", "lat")),
            P("lon"),
        ),
        out_specs=P(None, None, "lat", "lon"),
        check_vma=False,
    )
```
